512 devices in a mesh: tok: 128 (over z, y, core), rep: 4 (over x).
Axes of the slice: x: 4, y: 8, z: 8, core: 2. Of those that a mesh axis runs over, the one named last changes fastest.
Arguments:
- hidden: bfloat16 [12288, 1024], P(('tok', 'rep')), may hold values from -50 to 50
- norm_gain: bfloat16 [1024], replicated, may hold values from 0.5 to 1.5
- head_weight: bfloat16 [32128, 1024], P('tok'), may hold values from -3.75 to 3.75
- targets: int32 [12288], P(('tok', 'rep')), may hold values from 0 to 32127
- lengths: int32 [64], replicated, may hold values from 96 to 288, as said below
- padding_mask: int32 [12288], P(('tok', 'rep')), may hold values from 0 to 1, as said below
- owner_map: int32 [64], replicated, may hold values from 0 to 511, as said below
Outputs:
- logprob: float32 [12288], P(('tok', 'rep'))
- entropy: float32 [12288], P(('tok', 'rep'))
- request_table: float32 [512, 2, 2], P(('tok', 'rep'))
The draws below stay inside these ranges and needn't reach their ends.
Inputs may be any that keep to these rules, and one draw needn't show every extreme that they name: `lengths`: lengths sum to 12288; the largest is exactly 288. `padding_mask`: the last token of every sequence is live. Each device's block of 24 tokens holds at most 18 live tokens, and the first block exactly 18. `owner_map`: each device owns at most 2 requests, and some device exactly 2.
All inputs are finite; a program needn't handle non-finite values.
Results may differ from the reference program's by a relative error of at most 0.015.
The reference program's roundings to bfloat16 on the way (of `normed`) count: a program that leaves them out, or rounds other values in their place, can miss the bound.
Values may be sent and summed in bfloat16 or wider, within the bound.
No kernel may reach another device: no remote copies, remote signals or barrier semaphores. Data moves between devices by JAX's collectives and lax.ppermute only.
A program may use at most 64 MiB of HBM per device.

```python
import math
import jax
import jax.numpy as jnp
import numpy as np
from jax import lax

D = 1024
V = 32128
TOK_DEV = 24
LIVE_DEV = 18
SLOTS = 2
TOKENS = 12288
SEQS = 64
N_TOK = 128
N_REP = 4


def head_matrix(key):
    base_key = jax.random.fold_in(key, 101)
    base = jax.random.truncated_normal(jax.random.fold_in(base_key, 1), -5.0, 5.0, (D, V), jnp.float32)
    log_scale = jax.random.uniform(jax.random.fold_in(base_key, 2), (V,), jnp.float32, math.log(0.5), math.log(4.0))
    ramp = jnp.arange(V, dtype=jnp.float32) / V * math.log(3.0)
    matrix = base * jnp.exp(log_scale + ramp)[None, :] * (2.0 / math.sqrt(D))
    return matrix


def draw_head_weight(key, part):
    return head_matrix(key).T.astype(jnp.bfloat16)


def draw_hidden(key, part):
    row_key = jax.random.fold_in(key, 202)
    values = jax.random.truncated_normal(jax.random.fold_in(row_key, 1), -5.0, 5.0, (TOKENS, D), jnp.float32)
    row_scale = jnp.exp(jax.random.uniform(jax.random.fold_in(row_key, 2), (TOKENS,), jnp.float32, 0.0, math.log(10.0)))
    values = values * row_scale[:, None]
    return values.astype(jnp.bfloat16)


def layout_lengths(key):
    layout_key = jax.random.fold_in(key, 303)
    half_count = SEQS // 2
    average = TOKENS // SEQS
    reach = average // 2
    offset = jax.random.randint(jax.random.fold_in(layout_key, 1), (half_count,), -reach, reach + 1)
    offset = offset.at[0].set(reach)
    paired = jnp.stack([average + offset, average - offset], axis=1).reshape(SEQS)
    ordering = jax.random.permutation(jax.random.fold_in(layout_key, 2), SEQS)
    return (paired[ordering].astype(jnp.int32), layout_key)


def draw_lengths(key, part):
    lengths_drawn, layout_key = layout_lengths(key)
    return lengths_drawn


def draw_padding_mask(key, part):
    lengths_drawn, layout_key = layout_lengths(key)
    seq_ends = jnp.cumsum(lengths_drawn).astype(jnp.int32)
    is_end = jnp.zeros((TOKENS,), jnp.int32).at[seq_ends - 1].set(1)
    block_count = TOKENS // TOK_DEV
    end_block = is_end.reshape(block_count, TOK_DEV)
    has_end = jnp.sum(end_block, axis=1)
    keep_count = jax.random.randint(jax.random.fold_in(layout_key, 3), (block_count,), LIVE_DEV // 3, LIVE_DEV + 1) - has_end
    keep_count = keep_count.at[0].set(LIVE_DEV - has_end[0])
    scores = jax.random.randint(jax.random.fold_in(layout_key, 4), (block_count, TOK_DEV), 0, 1 << 20) * TOK_DEV
    scores = scores + jnp.arange(TOK_DEV, dtype=jnp.int32)[None, :] + end_block * (1 << 30)
    ranking = jnp.argsort(jnp.argsort(scores, axis=1), axis=1)
    live_row = (end_block == 1) | (ranking < keep_count[:, None])
    return live_row.reshape(TOKENS).astype(jnp.int32)


def draw_owner_map(key, part):
    owner_key = jax.random.fold_in(key, 404)
    device_total = N_TOK * N_REP
    devices_perm = jax.random.permutation(jax.random.fold_in(owner_key, 1), device_total).astype(jnp.int32)
    devices_perm = jnp.where(devices_perm == device_total - 1, devices_perm[0], devices_perm).at[0].set(device_total - 1)
    devices_perm = jnp.where(devices_perm == 0, devices_perm[1], devices_perm).at[1].set(0)
    seq_ids = jnp.arange(SEQS, dtype=jnp.int32)
    joined = jax.random.randint(jax.random.fold_in(owner_key, 2), (SEQS,), 0, 2)
    joined = joined.at[1].set(1)
    pair_owner = devices_perm[seq_ids // 2]
    lone_owner = devices_perm[SEQS // 2 + seq_ids]
    owners = jnp.where((seq_ids % 2 == 0) | (joined == 1), pair_owner, lone_owner)
    return owners.astype(jnp.int32)


def set_ends(result, rng, smallest, largest):
    index_at = [jax.random.randint(jax.random.fold_in(rng, axis), (), 0, length) for axis, length in enumerate(result.shape)]
    widest = result.shape.index(max(result.shape))
    beside = index_at[:widest] + [(index_at[widest] + 1) % result.shape[widest]] + index_at[widest + 1:]
    return result.at[tuple(index_at)].set(smallest).at[tuple(beside)].set(largest)


def rank_table(number_of, lean):
    weights = [(1 << 20) // math.isqrt(rank ** lean) + 1 for rank in range(1, number_of + 1)]
    scale = 1 + sum(weights) // (1 << 30)
    return np.cumsum(np.array([max(1, weight // scale) for weight in weights]))


def ranked(own_key, dims, count, slope):
    listing = rank_table(count, slope)
    pick = jax.random.randint(jax.random.fold_in(own_key, 1), dims, 0, int(listing[count - 1]))
    standing = jnp.searchsorted(jnp.asarray(listing, jnp.int32), pick, side="right")
    return jax.random.permutation(jax.random.fold_in(own_key, 2), count)[standing].astype(jnp.int32)


def setup_inputs(seed: int = 0) -> dict:
    arg_keys = jax.random.split(jax.random.key(seed), 8)
    return {
        "hidden": draw_hidden(jax.random.fold_in(arg_keys[7], 71), 0),
        "norm_gain": jnp.clip(1.0 + 0.1 * jax.random.normal(arg_keys[1], (D,), jnp.float32), 0.5, 1.5).astype(jnp.bfloat16),
        "head_weight": draw_head_weight(jax.random.fold_in(arg_keys[7], 71), 0),
        "targets": set_ends(ranked(arg_keys[3], (TOKENS,), V, 2), jax.random.fold_in(arg_keys[3], 3), 0, V - 1).astype(jnp.int32),
        "lengths": draw_lengths(jax.random.fold_in(arg_keys[7], 71), 0),
        "padding_mask": draw_padding_mask(jax.random.fold_in(arg_keys[7], 71), 0),
        "owner_map": draw_owner_map(jax.random.fold_in(arg_keys[7], 71), 0),
    }


EPSILON = 1e-06
NEG_FILL = -1e+30

def reference(hidden, norm_gain, head_weight, targets, lengths, padding_mask, owner_map):
    widened = hidden.astype(jnp.float32)
    mean_square = lax.optimization_barrier(jnp.mean(widened * widened, axis=1))
    normed = (widened * lax.rsqrt(mean_square + EPSILON)[:, None] * norm_gain.astype(jnp.float32)[None, :]).astype(jnp.bfloat16)
    state_norm = jnp.sqrt(mean_square)
    block_size = math.gcd(TOKENS, 512)
    vocab_ids = jnp.arange(V, dtype=jnp.int32)

    def one_block(operands):
        block_rows, block_ids = operands
        logits = lax.dot_general(block_rows, head_weight, (((1,), (1,)), ((), ())), preferred_element_type=jnp.float32)
        row_top = lax.optimization_barrier(jnp.max(logits, axis=1))
        weights = jnp.exp(logits - row_top[:, None])
        row_total = lax.optimization_barrier(jnp.sum(weights, axis=1))
        moment = lax.optimization_barrier(jnp.sum(weights * logits, axis=1))
        chosen = lax.optimization_barrier(jnp.sum(jnp.where(vocab_ids[None, :] == block_ids[:, None], logits, 0.0), axis=1))
        return (row_top, row_total, moment, chosen)
    block_count = TOKENS // block_size
    row_stats = lax.map(one_block, (normed.reshape(block_count, block_size, D), targets.reshape(block_count, block_size)))
    row_top, row_total, row_moment, row_chosen = (piece_stat.reshape(TOKENS) for piece_stat in row_stats)
    live_row = padding_mask == 1
    log_total = jnp.log(row_total)
    logprob = jnp.where(live_row, row_chosen - row_top - log_total, 0.0)
    entropy = jnp.where(live_row, row_top + log_total - row_moment / row_total, 0.0)
    seq_ends = jnp.cumsum(lengths).astype(jnp.int32)
    global_row = jnp.arange(TOKENS, dtype=jnp.int32)
    sequence_of = lax.optimization_barrier(jnp.sum((seq_ends[None, :] <= global_row[:, None]).astype(jnp.int32), axis=1))
    seq_ids = jnp.arange(SEQS, dtype=jnp.int32)
    member = (sequence_of[:, None] == seq_ids[None, :]) & live_row[:, None]
    request_max = lax.optimization_barrier(jnp.max(jnp.where(member, row_top[:, None], NEG_FILL), axis=0))
    request_norm = lax.optimization_barrier(jnp.sum(jnp.where(global_row[:, None] == seq_ends[None, :] - 1, state_norm[:, None], 0.0), axis=0))
    values = jnp.stack([request_max, request_norm], axis=1)
    earlier_same = (owner_map[None, :] == owner_map[:, None]) & (seq_ids[None, :] < seq_ids[:, None])
    slot_rank = lax.optimization_barrier(jnp.sum(earlier_same.astype(jnp.int32), axis=1))
    device_ids = jnp.arange(N_TOK * N_REP, dtype=jnp.int32)
    owner_hot = owner_map[:, None] == device_ids[None, :]
    slot_hot = slot_rank[:, None] == jnp.arange(SLOTS, dtype=jnp.int32)[None, :]
    both_hot = owner_hot[:, :, None, None] & slot_hot[:, None, :, None]
    request_table = lax.optimization_barrier(jnp.sum(jnp.where(both_hot, values[:, None, None, :], 0.0), axis=0))
    return (logprob, entropy, request_table)
```

```python
import jax
import jax.numpy as jnp
from jax import lax
from jax.sharding import PartitionSpec as P

SLOTS = 2


EPSILON = 1e-06
NEG_FILL = -1e30


def slice_stats(rows, ids, head_weight, vocab_ids):
    logits = lax.dot_general(
        rows, head_weight, (((2,), (1,)), ((), ())), preferred_element_type=jnp.float32
    )
    row_top = jnp.max(logits, axis=2)
    weights = jnp.exp(logits - row_top[:, :, None])
    row_total = jnp.sum(weights, axis=2)
    moment = jnp.sum(weights * logits, axis=2)
    chosen = jnp.sum(jnp.where(vocab_ids[None, None, :] == ids[:, :, None], logits, 0.0), axis=2)
    return row_top, row_total, moment, chosen


def shards(hidden, norm_gain, head_weight, targets, lengths, padding_mask, owner_map):
    tok_count = lax.axis_size("tok")
    rep_count = lax.axis_size("rep")
    tok_place = lax.axis_index("tok")
    rep_place = lax.axis_index("rep")
    local_rows, width = hidden.shape
    slice_width = head_weight.shape[0]
    seq_count = lengths.shape[0]

    widened = hidden.astype(jnp.float32)
    mean_square = jnp.mean(widened * widened, axis=1)
    normed = (
        widened * lax.rsqrt(mean_square + EPSILON)[:, None] * norm_gain.astype(jnp.float32)[None, :]
    ).astype(jnp.bfloat16)
    state_norm = jnp.sqrt(mean_square)
    live_row = padding_mask == 1

    meta = jnp.zeros((width,), jnp.float32)
    meta = meta.at[0:local_rows].set((targets // 256).astype(jnp.float32))
    meta = meta.at[local_rows:2 * local_rows].set((targets % 256).astype(jnp.float32))
    meta = meta.at[2 * local_rows:3 * local_rows].set(live_row.astype(jnp.float32))
    packet = jnp.concatenate([normed, meta.astype(jnp.bfloat16)[None, :]], axis=0)
    gathered = lax.all_gather(packet, "tok", axis=0)

    meta_all = gathered[:, local_rows, :].astype(jnp.float32)
    piece_ids = (meta_all[:, 0:local_rows] * 256.0 + meta_all[:, local_rows:2 * local_rows]).astype(jnp.int32)
    piece_live = meta_all[:, 2 * local_rows:3 * local_rows] > 0.5
    vocab_ids = tok_place * slice_width + jnp.arange(slice_width, dtype=jnp.int32)
    ids_full = jnp.concatenate([piece_ids, jnp.zeros((tok_count, 1), jnp.int32)], axis=1)
    top_p, total_p, moment_p, chosen_p = (
        part[:, :local_rows] for part in slice_stats(gathered, ids_full, head_weight, vocab_ids)
    )

    seq_ends = jnp.cumsum(lengths)
    seq_ids = jnp.arange(seq_count, dtype=jnp.int32)
    block_of = jnp.arange(tok_count, dtype=jnp.int32) * rep_count + rep_place
    piece_rows = block_of[:, None] * local_rows + jnp.arange(local_rows, dtype=jnp.int32)[None, :]
    piece_seq = jnp.sum((seq_ends[None, None, :] <= piece_rows[:, :, None]).astype(jnp.int32), axis=2)
    member = (piece_seq[:, :, None] == seq_ids[None, None, :]) & piece_live[:, :, None]
    part_max = jnp.max(jnp.where(member, top_p[:, :, None], NEG_FILL), axis=(0, 1))
    device_place = tok_place * rep_count + rep_place
    own_rows = device_place * local_rows + jnp.arange(local_rows, dtype=jnp.int32)
    part_norm = jnp.sum(
        jnp.where(own_rows[:, None] == seq_ends[None, :] - 1, state_norm[:, None], 0.0), axis=0
    )

    earlier_same = (owner_map[None, :] == owner_map[:, None]) & (seq_ids[None, :] < seq_ids[:, None])
    slot_rank = jnp.sum(earlier_same.astype(jnp.int32), axis=1)
    device_ids = jnp.arange(tok_count * rep_count, dtype=jnp.int32)
    slot_hot = (owner_map[:, None, None] == device_ids[None, :, None]) & (
        slot_rank[:, None, None] == jnp.arange(SLOTS, dtype=jnp.int32)[None, None, :]
    )
    req_max = jnp.max(jnp.where(slot_hot, part_max[:, None, None], NEG_FILL), axis=0)
    req_norm = jnp.sum(jnp.where(slot_hot, part_norm[:, None, None], 0.0), axis=0)
    req = jnp.stack([req_max, req_norm], axis=2).reshape(tok_count, rep_count * SLOTS * 2)

    stats = jnp.stack([top_p, total_p, moment_p, chosen_p], axis=2).reshape(tok_count, local_rows * 4)
    outgoing = jnp.concatenate([stats, req], axis=1)
    incoming = lax.all_to_all(outgoing, "tok", 0, 0, tiled=True)

    in_stats = incoming[:, : local_rows * 4].reshape(tok_count, local_rows, 4)
    tops = in_stats[:, :, 0]
    row_top = jnp.max(tops, axis=0)
    scale = jnp.exp(tops - row_top[None, :])
    row_total = jnp.sum(in_stats[:, :, 1] * scale, axis=0)
    row_moment = jnp.sum(in_stats[:, :, 2] * scale, axis=0)
    row_chosen = jnp.sum(in_stats[:, :, 3], axis=0)
    log_total = jnp.log(row_total)
    logprob = jnp.where(live_row, row_chosen - row_top - log_total, 0.0)
    entropy = jnp.where(live_row, row_top + log_total - row_moment / row_total, 0.0)

    in_req = incoming[:, local_rows * 4:].reshape(tok_count, rep_count, SLOTS, 2)
    rep_max = jnp.max(in_req[..., 0], axis=0)
    rep_norm = jnp.sum(in_req[..., 1], axis=0)
    rep_pair = jnp.stack([rep_max, rep_norm], axis=2)
    got = lax.all_to_all(rep_pair, "rep", 0, 0, tiled=True)
    final_max = jnp.max(got[..., 0], axis=0)
    final_norm = jnp.sum(got[..., 1], axis=0)
    has_slot = jnp.any(slot_hot[:, device_place, :], axis=0)
    request_table = jnp.where(
        has_slot[:, None], jnp.stack([final_max, final_norm], axis=1), 0.0
    )
    return (logprob, entropy, request_table[None])


def solution(mesh):
    return jax.shard_map(
        shards,
        mesh=mesh,
        in_specs=(
            P(("tok", "rep"), None),
            P(),
            P("tok", None),
            P(("tok", "rep")),
            P(),
            P(("tok", "rep")),
            P(),
        ),
        out_specs=(P(("tok", "rep")), P(("tok", "rep")), P(("tok", "rep"), None, None)),
        check_vma=False,
    )
```

```python
import jax
import jax.numpy as jnp
import numpy as np
from jax import lax
from jax.sharding import Mesh
from jax.sharding import PartitionSpec as P

SLOTS = 2


EPSILON = 1e-06
NEG_FILL = -1e30
AXES = ("z", "y", "c", "x")
PLANE = ("z", "y")
CHIP = ("c", "x")


def slice_stats(rows, ids, vocab, vocab_ids):
    logits = lax.dot_general(
        rows, vocab, (((rows.ndim - 1,), (1,)), ((), ())), preferred_element_type=jnp.float32
    )
    row_top = jnp.max(logits, axis=-1)
    weights = jnp.exp(logits - row_top[..., None])
    row_total = jnp.sum(weights, axis=-1)
    moment = jnp.sum(weights * logits, axis=-1)
    chosen = jnp.sum(jnp.where(vocab_ids == ids[..., None], logits, 0.0), axis=-1)
    return row_top, row_total, moment, chosen


def gather_by_sum(block, axis):
    count = lax.axis_size(axis)
    place = lax.axis_index(axis)
    buffer = jnp.zeros((count,) + block.shape, block.dtype)
    buffer = lax.dynamic_update_slice(buffer, block[None], (place,) + (0,) * block.ndim)
    return lax.psum(buffer, axis)


def shards(hidden, norm_gain, head_weight, targets, lengths, padding_mask, owner_map):
    nz, ny, nc, nx = (lax.axis_size(a) for a in AXES)
    z, y, c, x = (lax.axis_index(a) for a in AXES)
    plane_count = nz * ny
    chip_count = nc * nx
    local_rows, width = hidden.shape
    slice_width = head_weight.shape[0]
    seq_count = lengths.shape[0]
    tok_place = (z * ny + y) * nc + c
    device_place = tok_place * nx + x

    widened = hidden.astype(jnp.float32)
    mean_square = jnp.mean(widened * widened, axis=1)
    normed = (
        widened * lax.rsqrt(mean_square + EPSILON)[:, None] * norm_gain.astype(jnp.float32)[None, :]
    ).astype(jnp.bfloat16)
    state_norm = jnp.sqrt(mean_square)
    live_row = padding_mask == 1

    other_head = lax.ppermute(head_weight, "c", [(i, (i + 1) % nc) for i in range(nc)])
    other_place = (z * ny + y) * nc + (c + nc - 1) % nc
    vocab = jnp.concatenate([head_weight, other_head], axis=0)
    vocab_ids = jnp.concatenate(
        [
            tok_place * slice_width + jnp.arange(slice_width, dtype=jnp.int32),
            other_place * slice_width + jnp.arange(slice_width, dtype=jnp.int32),
        ]
    )

    meta = jnp.zeros((width,), jnp.float32)
    meta = meta.at[0:local_rows].set((targets // 256).astype(jnp.float32))
    meta = meta.at[local_rows:2 * local_rows].set((targets % 256).astype(jnp.float32))
    meta = meta.at[2 * local_rows:3 * local_rows].set(live_row.astype(jnp.float32))
    packet = jnp.concatenate([normed, meta.astype(jnp.bfloat16)[None, :]], axis=0)
    gathered = gather_by_sum(gather_by_sum(packet, "y"), "z")
    gathered = gathered.reshape(plane_count, local_rows + 1, width)

    meta_all = gathered[:, local_rows, :].astype(jnp.float32)
    piece_ids = (meta_all[:, 0:local_rows] * 256.0 + meta_all[:, local_rows:2 * local_rows]).astype(jnp.int32)
    piece_live = meta_all[:, 2 * local_rows:3 * local_rows] > 0.5
    ids_full = jnp.concatenate([piece_ids, jnp.zeros((plane_count, 1), jnp.int32)], axis=1)
    top_p, total_p, moment_p, chosen_p = (
        part[:, :local_rows] for part in slice_stats(gathered, ids_full, vocab, vocab_ids)
    )

    seq_ends = jnp.cumsum(lengths)
    seq_ids = jnp.arange(seq_count, dtype=jnp.int32)
    block_of = (jnp.arange(plane_count, dtype=jnp.int32) * nc + c) * nx + x
    piece_rows = block_of[:, None] * local_rows + jnp.arange(local_rows, dtype=jnp.int32)[None, :]
    piece_seq = jnp.sum((seq_ends[None, None, :] <= piece_rows[:, :, None]).astype(jnp.int32), axis=2)
    member = (piece_seq[:, :, None] == seq_ids[None, None, :]) & piece_live[:, :, None]
    part_max = jnp.max(jnp.where(member, top_p[:, :, None], NEG_FILL), axis=(0, 1))
    own_rows = device_place * local_rows + jnp.arange(local_rows, dtype=jnp.int32)
    part_norm = jnp.sum(
        jnp.where(own_rows[:, None] == seq_ends[None, :] - 1, state_norm[:, None], 0.0), axis=0
    )

    earlier_same = (owner_map[None, :] == owner_map[:, None]) & (seq_ids[None, :] < seq_ids[:, None])
    slot_rank = jnp.sum(earlier_same.astype(jnp.int32), axis=1)
    device_ids = jnp.arange(plane_count * chip_count, dtype=jnp.int32)
    slot_hot = (owner_map[:, None, None] == device_ids[None, :, None]) & (
        slot_rank[:, None, None] == jnp.arange(SLOTS, dtype=jnp.int32)[None, None, :]
    )
    req_max = jnp.max(jnp.where(slot_hot, part_max[:, None, None], NEG_FILL), axis=0)
    req_norm = jnp.sum(jnp.where(slot_hot, part_norm[:, None, None], 0.0), axis=0)
    req = jnp.stack([req_max, req_norm], axis=2).reshape(plane_count, chip_count * SLOTS * 2)

    stats = jnp.stack([top_p, total_p, moment_p, chosen_p], axis=2).reshape(plane_count, local_rows * 4)
    outgoing = jnp.concatenate([stats, req], axis=1)
    incoming = lax.all_to_all(outgoing, PLANE, 0, 0, tiled=True)

    in_stats = incoming[:, : local_rows * 4].reshape(plane_count, local_rows, 4)
    tops = in_stats[:, :, 0]
    row_top = jnp.max(tops, axis=0)
    scale = jnp.exp(tops - row_top[None, :])
    row_total = jnp.sum(in_stats[:, :, 1] * scale, axis=0)
    row_moment = jnp.sum(in_stats[:, :, 2] * scale, axis=0)
    row_chosen = jnp.sum(in_stats[:, :, 3], axis=0)
    log_total = jnp.log(row_total)
    logprob = jnp.where(live_row, row_chosen - row_top - log_total, 0.0)
    entropy = jnp.where(live_row, row_top + log_total - row_moment / row_total, 0.0)

    in_req = incoming[:, local_rows * 4:].reshape(plane_count, chip_count, SLOTS, 2)
    chip_max = jnp.max(in_req[..., 0], axis=0)
    chip_norm = jnp.sum(in_req[..., 1], axis=0)
    chip_pair = jnp.stack([chip_max, chip_norm], axis=2)
    got = lax.all_to_all(chip_pair, CHIP, 0, 0, tiled=True)
    final_max = jnp.max(got[..., 0], axis=0)
    final_norm = jnp.sum(got[..., 1], axis=0)
    has_slot = jnp.any(slot_hot[:, device_place, :], axis=0)
    request_table = jnp.where(
        has_slot[:, None], jnp.stack([final_max, final_norm], axis=1), 0.0
    )
    return (logprob, entropy, request_table[None])


def solution(mesh):
    tok_count, rep_count = mesh.devices.shape
    cores = 2
    side = int(round((tok_count // cores) ** 0.5))
    fine = Mesh(np.asarray(mesh.devices).reshape(side, tok_count // cores // side, cores, rep_count), AXES)
    tokens = P(AXES)
    return jax.shard_map(
        shards,
        mesh=fine,
        in_specs=(
            P(AXES, None),
            P(),
            P(("z", "y", "c"), None),
            tokens,
            P(),
            tokens,
            P(),
        ),
        out_specs=(tokens, tokens, P(AXES, None, None)),
        check_vma=False,
    )
```

```python
import jax
import jax.numpy as jnp
from jax import lax
from jax.sharding import PartitionSpec as P

SLOTS = 2


EPSILON = 1e-06
NEG_FILL = -1e30


def slice_stats(rows, ids, head_weight, vocab_ids):
    logits = lax.dot_general(
        head_weight, rows, (((1,), (1,)), ((), ())), preferred_element_type=jnp.float32
    )
    row_top = jnp.max(logits, axis=0)
    weights = jnp.exp(logits - row_top[None, :])
    row_total = jnp.sum(weights, axis=0)
    moment = jnp.sum(weights * logits, axis=0)
    chosen = jnp.sum(jnp.where(vocab_ids[:, None] == ids[None, :], logits, 0.0), axis=0)
    return row_top, row_total, moment, chosen


def shards(hidden, norm_gain, head_weight, targets, lengths, padding_mask, owner_map):
    tok_count = lax.axis_size("tok")
    rep_count = lax.axis_size("rep")
    tok_place = lax.axis_index("tok")
    rep_place = lax.axis_index("rep")
    local_rows, width = hidden.shape
    slice_width = head_weight.shape[0]
    seq_count = lengths.shape[0]

    widened = hidden.astype(jnp.float32)
    mean_square = jnp.mean(widened * widened, axis=1)
    normed = (
        widened * lax.rsqrt(mean_square + EPSILON)[:, None] * norm_gain.astype(jnp.float32)[None, :]
    ).astype(jnp.bfloat16)
    state_norm = jnp.sqrt(mean_square)
    live_row = padding_mask == 1

    pad_rows = 8
    meta = jnp.concatenate(
        [
            (targets // 256).astype(jnp.float32),
            (targets % 256).astype(jnp.float32),
            live_row.astype(jnp.float32),
            jnp.zeros((width - 3 * local_rows,), jnp.float32),
        ]
    )
    meta_rows = jnp.concatenate([meta[None, :], jnp.zeros((pad_rows - 1, width), jnp.float32)], axis=0)
    packet = jnp.concatenate([normed, meta_rows.astype(jnp.bfloat16)], axis=0)
    block_rows = local_rows + pad_rows
    gathered = lax.all_gather(packet, "tok", axis=0)

    meta_all = gathered[:, local_rows, :].astype(jnp.float32)
    piece_ids = (meta_all[:, 0:local_rows] * 256.0 + meta_all[:, local_rows:2 * local_rows]).astype(jnp.int32)
    piece_live = meta_all[:, 2 * local_rows:3 * local_rows] > 0.5
    vocab_ids = tok_place * slice_width + jnp.arange(slice_width, dtype=jnp.int32)
    ids_full = jnp.concatenate([piece_ids, jnp.zeros((tok_count, pad_rows), jnp.int32)], axis=1)
    flat_stats = slice_stats(
        gathered.reshape(tok_count * block_rows, width), ids_full.reshape(-1), head_weight, vocab_ids
    )
    top_p, total_p, moment_p, chosen_p = (
        part.reshape(tok_count, block_rows)[:, :local_rows] for part in flat_stats
    )

    seq_ends = jnp.cumsum(lengths)
    seq_ids = jnp.arange(seq_count, dtype=jnp.int32)
    block_of = jnp.arange(tok_count, dtype=jnp.int32) * rep_count + rep_place
    piece_rows = block_of[:, None] * local_rows + jnp.arange(local_rows, dtype=jnp.int32)[None, :]
    piece_seq = jnp.sum((seq_ends[None, None, :] <= piece_rows[:, :, None]).astype(jnp.int32), axis=2)
    member = (piece_seq[:, :, None] == seq_ids[None, None, :]) & piece_live[:, :, None]
    part_max = jnp.max(jnp.where(member, top_p[:, :, None], NEG_FILL), axis=(0, 1))
    device_place = tok_place * rep_count + rep_place
    own_rows = device_place * local_rows + jnp.arange(local_rows, dtype=jnp.int32)
    part_norm = jnp.sum(
        jnp.where(own_rows[:, None] == seq_ends[None, :] - 1, state_norm[:, None], 0.0), axis=0
    )

    earlier_same = (owner_map[None, :] == owner_map[:, None]) & (seq_ids[None, :] < seq_ids[:, None])
    slot_rank = jnp.sum(earlier_same.astype(jnp.int32), axis=1)
    device_ids = jnp.arange(tok_count * rep_count, dtype=jnp.int32)
    slot_hot = (owner_map[:, None, None] == device_ids[None, :, None]) & (
        slot_rank[:, None, None] == jnp.arange(SLOTS, dtype=jnp.int32)[None, None, :]
    )
    req_max = jnp.max(jnp.where(slot_hot, part_max[:, None, None], NEG_FILL), axis=0)
    req_norm = jnp.sum(jnp.where(slot_hot, part_norm[:, None, None], 0.0), axis=0)
    req = jnp.stack([req_max, req_norm], axis=2).reshape(tok_count, rep_count * SLOTS * 2)

    stats = jnp.stack([top_p, total_p, moment_p, chosen_p], axis=2).reshape(tok_count, local_rows * 4)
    outgoing = jnp.concatenate([stats, req], axis=1)
    incoming = lax.all_to_all(outgoing, "tok", 0, 0, tiled=True)

    in_stats = incoming[:, : local_rows * 4].reshape(tok_count, local_rows, 4)
    tops = in_stats[:, :, 0]
    row_top = jnp.max(tops, axis=0)
    scale = jnp.exp(tops - row_top[None, :])
    row_total = jnp.sum(in_stats[:, :, 1] * scale, axis=0)
    row_moment = jnp.sum(in_stats[:, :, 2] * scale, axis=0)
    row_chosen = jnp.sum(in_stats[:, :, 3], axis=0)
    log_total = jnp.log(row_total)
    logprob = jnp.where(live_row, row_chosen - row_top - log_total, 0.0)
    entropy = jnp.where(live_row, row_top + log_total - row_moment / row_total, 0.0)

    in_req = incoming[:, local_rows * 4:].reshape(tok_count, rep_count, SLOTS, 2)
    rep_max = jnp.max(in_req[..., 0], axis=0)
    rep_norm = jnp.sum(in_req[..., 1], axis=0)
    rep_pair = jnp.stack([rep_max, rep_norm], axis=2)
    got = lax.all_to_all(rep_pair, "rep", 0, 0, tiled=True)
    final_max = jnp.max(got[..., 0], axis=0)
    final_norm = jnp.sum(got[..., 1], axis=0)
    has_slot = jnp.any(slot_hot[:, device_place, :], axis=0)
    request_table = jnp.where(
        has_slot[:, None], jnp.stack([final_max, final_norm], axis=1), 0.0
    )
    return (logprob, entropy, request_table[None])


def solution(mesh):
    return jax.shard_map(
        shards,
        mesh=mesh,
        in_specs=(
            P(("tok", "rep"), None),
            P(),
            P("tok", None),
            P(("tok", "rep")),
            P(),
            P(("tok", "rep")),
            P(),
        ),
        out_specs=(P(("tok", "rep")), P(("tok", "rep")), P(("tok", "rep"), None, None)),
        check_vma=False,
    )
```

```python
import jax
import jax.numpy as jnp
from jax import lax
from jax.experimental import pallas as pl
from jax.experimental.pallas import tpu as pltpu
from jax.sharding import PartitionSpec as P

SLOTS = 2


EPSILON = 1e-06
NEG_FILL = -1e30


TILE = 512
VOCAB_PAD = 256


def stats_kernel(head_ref, vocab_ref, ids_ref, rows_ref, out_ref):
    logits = lax.dot_general(
        head_ref[...], rows_ref[...], (((1,), (1,)), ((), ())), preferred_element_type=jnp.float32
    )
    real = vocab_ref[...] >= 0
    logits = jnp.where(real, logits, -jnp.inf)
    row_top = jnp.max(logits, axis=0, keepdims=True)
    weights = jnp.where(real, jnp.exp(logits - row_top), 0.0)
    row_total = jnp.sum(weights, axis=0, keepdims=True)
    moment = jnp.sum(jnp.where(real, weights * logits, 0.0), axis=0, keepdims=True)
    chosen = jnp.sum(jnp.where(vocab_ref[...] == ids_ref[...], logits, 0.0), axis=0, keepdims=True)
    out_ref[...] = jnp.concatenate(
        [row_top, row_total, moment, chosen, jnp.zeros((4, row_top.shape[1]), jnp.float32)], axis=0
    )


def slice_stats(rows, ids, head_weight, vocab_ids):
    count, width = rows.shape
    tile = TILE if count % TILE == 0 else count
    slice_width = head_weight.shape[0]
    head = jnp.concatenate(
        [head_weight, jnp.zeros((VOCAB_PAD - slice_width, width), head_weight.dtype)], axis=0
    )
    vocab = jnp.concatenate(
        [vocab_ids, jnp.full((VOCAB_PAD - slice_width,), -1, jnp.int32)]
    )[:, None]
    out = pl.pallas_call(
        stats_kernel,
        grid=(count // tile,),
        in_specs=[
            pl.BlockSpec((VOCAB_PAD, width), lambda i: (0, 0)),
            pl.BlockSpec((VOCAB_PAD, 1), lambda i: (0, 0)),
            pl.BlockSpec((1, tile), lambda i: (0, i)),
            pl.BlockSpec((tile, width), lambda i: (i, 0)),
        ],
        out_specs=pl.BlockSpec((8, tile), lambda i: (0, i)),
        out_shape=jax.ShapeDtypeStruct((8, count), jnp.float32),
        cost_estimate=pl.CostEstimate(
            flops=2 * VOCAB_PAD * width * count,
            transcendentals=VOCAB_PAD * count,
            bytes_accessed=count * width * 2 + VOCAB_PAD * width * 2 + count * 36,
        ),
    )(head, vocab, ids[None, :], rows)
    return out[0], out[1], out[2], out[3]


def shards(hidden, norm_gain, head_weight, targets, lengths, padding_mask, owner_map):
    tok_count = lax.axis_size("tok")
    rep_count = lax.axis_size("rep")
    tok_place = lax.axis_index("tok")
    rep_place = lax.axis_index("rep")
    local_rows, width = hidden.shape
    slice_width = head_weight.shape[0]
    seq_count = lengths.shape[0]

    widened = hidden.astype(jnp.float32)
    mean_square = jnp.mean(widened * widened, axis=1)
    normed = (
        widened * lax.rsqrt(mean_square + EPSILON)[:, None] * norm_gain.astype(jnp.float32)[None, :]
    ).astype(jnp.bfloat16)
    state_norm = jnp.sqrt(mean_square)
    live_row = padding_mask == 1

    pad_rows = 8
    meta = jnp.concatenate(
        [
            (targets // 256).astype(jnp.float32),
            (targets % 256).astype(jnp.float32),
            live_row.astype(jnp.float32),
            jnp.zeros((width - 3 * local_rows,), jnp.float32),
        ]
    )
    meta_rows = jnp.concatenate([meta[None, :], jnp.zeros((pad_rows - 1, width), jnp.float32)], axis=0)
    packet = jnp.concatenate([normed, meta_rows.astype(jnp.bfloat16)], axis=0)
    block_rows = local_rows + pad_rows
    gathered = lax.all_gather(packet, "tok", axis=0)

    meta_all = gathered[:, local_rows, :].astype(jnp.float32)
    piece_ids = (meta_all[:, 0:local_rows] * 256.0 + meta_all[:, local_rows:2 * local_rows]).astype(jnp.int32)
    piece_live = meta_all[:, 2 * local_rows:3 * local_rows] > 0.5
    vocab_ids = tok_place * slice_width + jnp.arange(slice_width, dtype=jnp.int32)
    ids_full = jnp.concatenate([piece_ids, jnp.zeros((tok_count, pad_rows), jnp.int32)], axis=1)
    flat_stats = slice_stats(
        gathered.reshape(tok_count * block_rows, width), ids_full.reshape(-1), head_weight, vocab_ids
    )
    top_p, total_p, moment_p, chosen_p = (
        part.reshape(tok_count, block_rows)[:, :local_rows] for part in flat_stats
    )

    seq_ends = jnp.cumsum(lengths)
    seq_ids = jnp.arange(seq_count, dtype=jnp.int32)
    block_of = jnp.arange(tok_count, dtype=jnp.int32) * rep_count + rep_place
    piece_rows = block_of[:, None] * local_rows + jnp.arange(local_rows, dtype=jnp.int32)[None, :]
    piece_seq = jnp.sum((seq_ends[None, None, :] <= piece_rows[:, :, None]).astype(jnp.int32), axis=2)
    member = (piece_seq[:, :, None] == seq_ids[None, None, :]) & piece_live[:, :, None]
    part_max = jnp.max(jnp.where(member, top_p[:, :, None], NEG_FILL), axis=(0, 1))
    device_place = tok_place * rep_count + rep_place
    own_rows = device_place * local_rows + jnp.arange(local_rows, dtype=jnp.int32)
    part_norm = jnp.sum(
        jnp.where(own_rows[:, None] == seq_ends[None, :] - 1, state_norm[:, None], 0.0), axis=0
    )

    earlier_same = (owner_map[None, :] == owner_map[:, None]) & (seq_ids[None, :] < seq_ids[:, None])
    slot_rank = jnp.sum(earlier_same.astype(jnp.int32), axis=1)
    device_ids = jnp.arange(tok_count * rep_count, dtype=jnp.int32)
    slot_hot = (owner_map[:, None, None] == device_ids[None, :, None]) & (
        slot_rank[:, None, None] == jnp.arange(SLOTS, dtype=jnp.int32)[None, None, :]
    )
    req_max = jnp.max(jnp.where(slot_hot, part_max[:, None, None], NEG_FILL), axis=0)
    req_norm = jnp.sum(jnp.where(slot_hot, part_norm[:, None, None], 0.0), axis=0)
    req = jnp.stack([req_max, req_norm], axis=2).reshape(tok_count, rep_count * SLOTS * 2)

    stats = jnp.stack([top_p, total_p, moment_p, chosen_p], axis=2).reshape(tok_count, local_rows * 4)
    outgoing = jnp.concatenate([stats, req], axis=1)
    incoming = lax.all_to_all(outgoing, "tok", 0, 0, tiled=True)

    in_stats = incoming[:, : local_rows * 4].reshape(tok_count, local_rows, 4)
    tops = in_stats[:, :, 0]
    row_top = jnp.max(tops, axis=0)
    scale = jnp.exp(tops - row_top[None, :])
    row_total = jnp.sum(in_stats[:, :, 1] * scale, axis=0)
    row_moment = jnp.sum(in_stats[:, :, 2] * scale, axis=0)
    row_chosen = jnp.sum(in_stats[:, :, 3], axis=0)
    log_total = jnp.log(row_total)
    logprob = jnp.where(live_row, row_chosen - row_top - log_total, 0.0)
    entropy = jnp.where(live_row, row_top + log_total - row_moment / row_total, 0.0)

    in_req = incoming[:, local_rows * 4:].reshape(tok_count, rep_count, SLOTS, 2)
    rep_max = jnp.max(in_req[..., 0], axis=0)
    rep_norm = jnp.sum(in_req[..., 1], axis=0)
    rep_pair = jnp.stack([rep_max, rep_norm], axis=2)
    got = lax.all_to_all(rep_pair, "rep", 0, 0, tiled=True)
    final_max = jnp.max(got[..., 0], axis=0)
    final_norm = jnp.sum(got[..., 1], axis=0)
    has_slot = jnp.any(slot_hot[:, device_place, :], axis=0)
    request_table = jnp.where(
        has_slot[:, None], jnp.stack([final_max, final_norm], axis=1), 0.0
    )
    return (logprob, entropy, request_table[None])


def solution(mesh):
    return jax.shard_map(
        shards,
        mesh=mesh,
        in_specs=(
            P(("tok", "rep"), None),
            P(),
            P("tok", None),
            P(("tok", "rep")),
            P(),
            P(("tok", "rep")),
            P(),
        ),
        out_specs=(P(("tok", "rep")), P(("tok", "rep")), P(("tok", "rep"), None, None)),
        check_vma=False,
    )
```

```python
import jax
import jax.numpy as jnp
from jax import lax
from jax.experimental import pallas as pl
from jax.experimental.pallas import tpu as pltpu
from jax.sharding import PartitionSpec as P

SLOTS = 2


EPSILON = 1e-06
NEG_FILL = -1e30


TILE = 512
VOCAB_PAD = 256


def stats_kernel(head_ref, vocab_ref, ids_ref, rows_ref, out_ref):
    logits = lax.dot_general(
        head_ref[...], rows_ref[...], (((1,), (1,)), ((), ())), preferred_element_type=jnp.float32
    )
    real = vocab_ref[...] >= 0
    logits = jnp.where(real, logits, -jnp.inf)
    row_top = jnp.max(logits, axis=0, keepdims=True)
    weights = jnp.where(real, jnp.exp(logits - row_top), 0.0)
    row_total = jnp.sum(weights, axis=0, keepdims=True)
    moment = jnp.sum(jnp.where(real, weights * logits, 0.0), axis=0, keepdims=True)
    chosen = jnp.sum(jnp.where(vocab_ref[...] == ids_ref[...], logits, 0.0), axis=0, keepdims=True)
    out_ref[...] = jnp.concatenate(
        [row_top, row_total, moment, chosen, jnp.zeros((4, row_top.shape[1]), jnp.float32)], axis=0
    )


def slice_stats(rows, ids, head_weight, vocab_ids):
    count, width = rows.shape
    tile = TILE if count % TILE == 0 else count
    slice_width = head_weight.shape[0]
    head = jnp.concatenate(
        [head_weight, jnp.zeros((VOCAB_PAD - slice_width, width), head_weight.dtype)], axis=0
    )
    vocab = jnp.concatenate(
        [vocab_ids, jnp.full((VOCAB_PAD - slice_width,), -1, jnp.int32)]
    )[:, None]
    out = pl.pallas_call(
        stats_kernel,
        grid=(count // tile,),
        in_specs=[
            pl.BlockSpec((VOCAB_PAD, width), lambda i: (0, 0)),
            pl.BlockSpec((VOCAB_PAD, 1), lambda i: (0, 0)),
            pl.BlockSpec((1, tile), lambda i: (0, i)),
            pl.BlockSpec((tile, width), lambda i: (i, 0)),
        ],
        out_specs=pl.BlockSpec((8, tile), lambda i: (0, i)),
        out_shape=jax.ShapeDtypeStruct((8, count), jnp.float32),
        cost_estimate=pl.CostEstimate(
            flops=2 * VOCAB_PAD * width * count,
            transcendentals=VOCAB_PAD * count,
            bytes_accessed=count * width * 2 + VOCAB_PAD * width * 2 + count * 36,
        ),
    )(head, vocab, ids[None, :], rows)
    return out[0], out[1], out[2], out[3]


def shards(hidden, norm_gain, head_weight, targets, lengths, padding_mask, owner_map):
    tok_count = lax.axis_size("tok")
    rep_count = lax.axis_size("rep")
    tok_place = lax.axis_index("tok")
    rep_place = lax.axis_index("rep")
    local_rows, width = hidden.shape
    slice_width = head_weight.shape[0]
    seq_count = lengths.shape[0]

    widened = hidden.astype(jnp.float32)
    mean_square = jnp.mean(widened * widened, axis=1)
    normed = (
        widened * lax.rsqrt(mean_square + EPSILON)[:, None] * norm_gain.astype(jnp.float32)[None, :]
    ).astype(jnp.bfloat16)
    state_norm = jnp.sqrt(mean_square)
    live_row = padding_mask == 1

    gathered = lax.all_gather(normed, "tok", axis=0, tiled=True)
    meta = lax.all_gather(jnp.stack([targets, padding_mask]), "tok", axis=0)
    piece_ids = meta[:, 0, :]
    piece_live = meta[:, 1, :] == 1
    vocab_ids = tok_place * slice_width + jnp.arange(slice_width, dtype=jnp.int32)
    flat_stats = slice_stats(gathered, piece_ids.reshape(-1), head_weight, vocab_ids)
    top_p, total_p, moment_p, chosen_p = (part.reshape(tok_count, local_rows) for part in flat_stats)

    seq_ends = jnp.cumsum(lengths)
    seq_ids = jnp.arange(seq_count, dtype=jnp.int32)
    block_of = jnp.arange(tok_count, dtype=jnp.int32) * rep_count + rep_place
    piece_rows = block_of[:, None] * local_rows + jnp.arange(local_rows, dtype=jnp.int32)[None, :]
    piece_seq = jnp.sum((seq_ends[None, None, :] <= piece_rows[:, :, None]).astype(jnp.int32), axis=2)
    member = (piece_seq[:, :, None] == seq_ids[None, None, :]) & piece_live[:, :, None]
    part_max = jnp.max(jnp.where(member, top_p[:, :, None], NEG_FILL), axis=(0, 1))
    device_place = tok_place * rep_count + rep_place
    own_rows = device_place * local_rows + jnp.arange(local_rows, dtype=jnp.int32)
    part_norm = jnp.sum(
        jnp.where(own_rows[:, None] == seq_ends[None, :] - 1, state_norm[:, None], 0.0), axis=0
    )

    earlier_same = (owner_map[None, :] == owner_map[:, None]) & (seq_ids[None, :] < seq_ids[:, None])
    slot_rank = jnp.sum(earlier_same.astype(jnp.int32), axis=1)
    device_ids = jnp.arange(tok_count * rep_count, dtype=jnp.int32)
    slot_hot = (owner_map[:, None, None] == device_ids[None, :, None]) & (
        slot_rank[:, None, None] == jnp.arange(SLOTS, dtype=jnp.int32)[None, None, :]
    )
    req_max = jnp.max(jnp.where(slot_hot, part_max[:, None, None], NEG_FILL), axis=0)
    req_norm = jnp.sum(jnp.where(slot_hot, part_norm[:, None, None], 0.0), axis=0)
    req = jnp.stack([req_max, req_norm], axis=2).reshape(tok_count, rep_count * SLOTS * 2)

    stats = jnp.stack([top_p, total_p, moment_p, chosen_p], axis=2).reshape(tok_count, local_rows * 4)
    outgoing = jnp.concatenate([stats, req], axis=1)
    incoming = lax.all_to_all(outgoing, "tok", 0, 0, tiled=True)

    in_stats = incoming[:, : local_rows * 4].reshape(tok_count, local_rows, 4)
    tops = in_stats[:, :, 0]
    row_top = jnp.max(tops, axis=0)
    scale = jnp.exp(tops - row_top[None, :])
    row_total = jnp.sum(in_stats[:, :, 1] * scale, axis=0)
    row_moment = jnp.sum(in_stats[:, :, 2] * scale, axis=0)
    row_chosen = jnp.sum(in_stats[:, :, 3], axis=0)
    log_total = jnp.log(row_total)
    logprob = jnp.where(live_row, row_chosen - row_top - log_total, 0.0)
    entropy = jnp.where(live_row, row_top + log_total - row_moment / row_total, 0.0)

    in_req = incoming[:, local_rows * 4:].reshape(tok_count, rep_count, SLOTS, 2)
    rep_max = jnp.max(in_req[..., 0], axis=0)
    rep_norm = jnp.sum(in_req[..., 1], axis=0)
    rep_pair = jnp.stack([rep_max, rep_norm], axis=2)
    got = lax.all_to_all(rep_pair, "rep", 0, 0, tiled=True)
    final_max = jnp.max(got[..., 0], axis=0)
    final_norm = jnp.sum(got[..., 1], axis=0)
    has_slot = jnp.any(slot_hot[:, device_place, :], axis=0)
    request_table = jnp.where(
        has_slot[:, None], jnp.stack([final_max, final_norm], axis=1), 0.0
    )
    return (logprob, entropy, request_table[None])


def solution(mesh):
    return jax.shard_map(
        shards,
        mesh=mesh,
        in_specs=(
            P(("tok", "rep"), None),
            P(),
            P("tok", None),
            P(("tok", "rep")),
            P(),
            P(("tok", "rep")),
            P(),
        ),
        out_specs=(P(("tok", "rep")), P(("tok", "rep")), P(("tok", "rep"), None, None)),
        check_vma=False,
    )
```

```python
import jax
import jax.numpy as jnp
from jax import lax
from jax.experimental import pallas as pl
from jax.experimental.pallas import tpu as pltpu
from jax.sharding import PartitionSpec as P

SLOTS = 2


EPSILON = 1e-06
NEG_FILL = -1e30


TILE = 512
VOCAB_PAD = 256


def stats_kernel(head_ref, vocab_ref, ids_ref, rows_ref, out_ref):
    logits = lax.dot_general(
        head_ref[...], rows_ref[...], (((1,), (1,)), ((), ())), preferred_element_type=jnp.float32
    )
    real = vocab_ref[...] >= 0
    logits = jnp.where(real, logits, -jnp.inf)
    row_top = jnp.max(logits, axis=0, keepdims=True)
    weights = jnp.where(real, jnp.exp(logits - row_top), 0.0)
    row_total = jnp.sum(weights, axis=0, keepdims=True)
    moment = jnp.sum(jnp.where(real, weights * logits, 0.0), axis=0, keepdims=True)
    chosen = jnp.sum(jnp.where(vocab_ref[...] == ids_ref[...], logits, 0.0), axis=0, keepdims=True)
    out_ref[...] = jnp.concatenate(
        [row_top, row_total, moment, chosen, jnp.zeros((4, row_top.shape[1]), jnp.float32)], axis=0
    )


def slice_stats(rows, ids, head_weight, vocab_ids):
    count, width = rows.shape
    tile = TILE if count % TILE == 0 else count
    slice_width = head_weight.shape[0]
    head = jnp.concatenate(
        [head_weight, jnp.zeros((VOCAB_PAD - slice_width, width), head_weight.dtype)], axis=0
    )
    vocab = jnp.concatenate(
        [vocab_ids, jnp.full((VOCAB_PAD - slice_width,), -1, jnp.int32)]
    )[:, None]
    out = pl.pallas_call(
        stats_kernel,
        grid=(count // tile,),
        in_specs=[
            pl.BlockSpec((VOCAB_PAD, width), lambda i: (0, 0)),
            pl.BlockSpec((VOCAB_PAD, 1), lambda i: (0, 0)),
            pl.BlockSpec((1, tile), lambda i: (0, i)),
            pl.BlockSpec((tile, width), lambda i: (i, 0)),
        ],
        out_specs=pl.BlockSpec((8, tile), lambda i: (0, i)),
        out_shape=jax.ShapeDtypeStruct((8, count), jnp.float32),
        cost_estimate=pl.CostEstimate(
            flops=2 * VOCAB_PAD * width * count,
            transcendentals=VOCAB_PAD * count,
            bytes_accessed=count * width * 2 + VOCAB_PAD * width * 2 + count * 36,
        ),
    )(head, vocab, ids[None, :], rows)
    return out[0], out[1], out[2], out[3]


def shards(hidden, norm_gain, head_weight, targets, lengths, padding_mask, owner_map):
    tok_count = lax.axis_size("tok")
    rep_count = lax.axis_size("rep")
    tok_place = lax.axis_index("tok")
    rep_place = lax.axis_index("rep")
    local_rows, width = hidden.shape
    slice_width = head_weight.shape[0]
    seq_count = lengths.shape[0]

    widened = hidden.astype(jnp.float32)
    mean_square = jnp.mean(widened * widened, axis=1)
    normed = (
        widened * lax.rsqrt(mean_square + EPSILON)[:, None] * norm_gain.astype(jnp.float32)[None, :]
    ).astype(jnp.bfloat16)
    state_norm = jnp.sqrt(mean_square)
    live_row = padding_mask == 1

    gathered = lax.all_gather(normed, "tok", axis=0, tiled=True)
    meta = lax.all_gather(jnp.stack([targets, padding_mask]), "tok", axis=0)
    piece_ids = meta[:, 0, :]
    piece_live = meta[:, 1, :] == 1
    vocab_ids = tok_place * slice_width + jnp.arange(slice_width, dtype=jnp.int32)
    flat_stats = slice_stats(gathered, piece_ids.reshape(-1), head_weight, vocab_ids)
    top_p, total_p, moment_p, chosen_p = (part.reshape(tok_count, local_rows) for part in flat_stats)

    seq_ends = jnp.cumsum(lengths)
    seq_ids = jnp.arange(seq_count, dtype=jnp.int32)
    block_of = jnp.arange(tok_count, dtype=jnp.int32) * rep_count + rep_place
    piece_rows = block_of[:, None] * local_rows + jnp.arange(local_rows, dtype=jnp.int32)[None, :]
    piece_seq = jnp.sum((seq_ends[None, None, :] <= piece_rows[:, :, None]).astype(jnp.int32), axis=2)
    member = (piece_seq[:, :, None] == seq_ids[None, None, :]) & piece_live[:, :, None]
    part_max = jnp.max(jnp.where(member, top_p[:, :, None], NEG_FILL), axis=(0, 1))
    device_place = tok_place * rep_count + rep_place
    own_rows = device_place * local_rows + jnp.arange(local_rows, dtype=jnp.int32)
    part_norm = jnp.sum(
        jnp.where(own_rows[:, None] == seq_ends[None, :] - 1, state_norm[:, None], 0.0), axis=0
    )

    earlier_same = (owner_map[None, :] == owner_map[:, None]) & (seq_ids[None, :] < seq_ids[:, None])
    slot_rank = jnp.sum(earlier_same.astype(jnp.int32), axis=1)
    device_ids = jnp.arange(tok_count * rep_count, dtype=jnp.int32)
    slot_hot = (owner_map[:, None, None] == device_ids[None, :, None]) & (
        slot_rank[:, None, None] == jnp.arange(SLOTS, dtype=jnp.int32)[None, None, :]
    )
    req_max = jnp.max(jnp.where(slot_hot, part_max[:, None, None], NEG_FILL), axis=0)
    req_norm = jnp.sum(jnp.where(slot_hot, part_norm[:, None, None], 0.0), axis=0)
    req = jnp.stack([req_max, req_norm], axis=2).reshape(tok_count, rep_count * SLOTS * 2)

    stats = jnp.stack([top_p, total_p, moment_p, chosen_p], axis=2).reshape(tok_count, local_rows * 4)
    outgoing = jnp.concatenate([stats, req], axis=1)
    incoming = lax.all_to_all(outgoing, "tok", 0, 0, tiled=True)

    in_stats = incoming[:, : local_rows * 4].reshape(tok_count, local_rows, 4)
    tops = in_stats[:, :, 0]
    row_top = jnp.max(tops, axis=0)
    scale = jnp.exp(tops - row_top[None, :])
    row_total = jnp.sum(in_stats[:, :, 1] * scale, axis=0)
    row_moment = jnp.sum(in_stats[:, :, 2] * scale, axis=0)
    row_chosen = jnp.sum(in_stats[:, :, 3], axis=0)
    log_total = jnp.log(row_total)
    logprob = jnp.where(live_row, row_chosen - row_top - log_total, 0.0)
    entropy = jnp.where(live_row, row_top + log_total - row_moment / row_total, 0.0)

    in_req = incoming[:, local_rows * 4:].reshape(tok_count, rep_count, SLOTS, 2)
    rep_max = jnp.max(in_req[..., 0], axis=0)
    rep_norm = jnp.sum(in_req[..., 1], axis=0)
    rep_pair = jnp.stack([rep_max, rep_norm], axis=2)
    rep_count_static = rep_pair.shape[0]
    shares = [lax.dynamic_index_in_dim(rep_pair, rep_place, 0, keepdims=False)]
    for shift in range(1, rep_count_static):
        share = lax.dynamic_index_in_dim(rep_pair, (rep_place + shift) % rep_count, 0, keepdims=False)
        pairs = [(i, (i + shift) % rep_count_static) for i in range(rep_count_static)]
        shares.append(lax.ppermute(share, "rep", pairs))
    got = jnp.stack(shares)
    final_max = jnp.max(got[..., 0], axis=0)
    final_norm = jnp.sum(got[..., 1], axis=0)
    has_slot = jnp.any(slot_hot[:, device_place, :], axis=0)
    request_table = jnp.where(
        has_slot[:, None], jnp.stack([final_max, final_norm], axis=1), 0.0
    )
    return (logprob, entropy, request_table[None])


def solution(mesh):
    return jax.shard_map(
        shards,
        mesh=mesh,
        in_specs=(
            P(("tok", "rep"), None),
            P(),
            P("tok", None),
            P(("tok", "rep")),
            P(),
            P(("tok", "rep")),
            P(),
        ),
        out_specs=(P(("tok", "rep")), P(("tok", "rep")), P(("tok", "rep"), None, None)),
        check_vma=False,
    )
```

```python
import jax
import jax.numpy as jnp
from jax import lax
from jax.experimental import pallas as pl
from jax.experimental.pallas import tpu as pltpu
from jax.sharding import PartitionSpec as P

SLOTS = 2


EPSILON = 1e-06
NEG_FILL = -1e30


TILE = 512
VOCAB_PAD = 256


def stats_kernel(head_ref, vocab_ref, ids_ref, rows_ref, out_ref):
    logits = jnp.dot(rows_ref[...], head_ref[...], preferred_element_type=jnp.float32)
    real = vocab_ref[...] >= 0
    logits = jnp.where(real, logits, -jnp.inf)
    row_top = jnp.max(logits, axis=1, keepdims=True)
    weights = jnp.where(real, jnp.exp(logits - row_top), 0.0)
    row_total = jnp.sum(weights, axis=1, keepdims=True)
    moment = jnp.sum(jnp.where(real, weights * logits, 0.0), axis=1, keepdims=True)
    chosen = jnp.sum(jnp.where(vocab_ref[...] == ids_ref[...], logits, 0.0), axis=1, keepdims=True)
    lane = lax.broadcasted_iota(jnp.int32, out_ref.shape, 1)
    out_ref[...] = jnp.where(
        lane == 0, row_top, jnp.where(lane == 1, row_total, jnp.where(lane == 2, moment, jnp.where(lane == 3, chosen, 0.0)))
    )


def slice_stats(rows, ids, head_weight, vocab_ids):
    count, width = rows.shape
    tile = TILE if count % TILE == 0 else count
    slice_width = head_weight.shape[0]
    head = jnp.concatenate(
        [head_weight, jnp.zeros((VOCAB_PAD - slice_width, width), head_weight.dtype)], axis=0
    ).T
    vocab = jnp.concatenate(
        [vocab_ids, jnp.full((VOCAB_PAD - slice_width,), -1, jnp.int32)]
    )[None, :]
    out = pl.pallas_call(
        stats_kernel,
        grid=(count // tile,),
        in_specs=[
            pl.BlockSpec((width, VOCAB_PAD), lambda i: (0, 0)),
            pl.BlockSpec((1, VOCAB_PAD), lambda i: (0, 0)),
            pl.BlockSpec((tile, 1), lambda i: (i, 0)),
            pl.BlockSpec((tile, width), lambda i: (i, 0)),
        ],
        out_specs=pl.BlockSpec((tile, 128), lambda i: (i, 0)),
        out_shape=jax.ShapeDtypeStruct((count, 128), jnp.float32),
        cost_estimate=pl.CostEstimate(
            flops=2 * VOCAB_PAD * width * count,
            transcendentals=VOCAB_PAD * count,
            bytes_accessed=count * width * 2 + VOCAB_PAD * width * 2 + count * 516,
        ),
    )(head, vocab, ids[:, None], rows)
    return out[:, 0], out[:, 1], out[:, 2], out[:, 3]


def shards(hidden, norm_gain, head_weight, targets, lengths, padding_mask, owner_map):
    tok_count = lax.axis_size("tok")
    rep_count = lax.axis_size("rep")
    tok_place = lax.axis_index("tok")
    rep_place = lax.axis_index("rep")
    local_rows, width = hidden.shape
    slice_width = head_weight.shape[0]
    seq_count = lengths.shape[0]

    widened = hidden.astype(jnp.float32)
    mean_square = jnp.mean(widened * widened, axis=1)
    normed = (
        widened * lax.rsqrt(mean_square + EPSILON)[:, None] * norm_gain.astype(jnp.float32)[None, :]
    ).astype(jnp.bfloat16)
    state_norm = jnp.sqrt(mean_square)
    live_row = padding_mask == 1

    gathered = lax.all_gather(normed, "tok", axis=0, tiled=True)
    meta = lax.all_gather(jnp.stack([targets, padding_mask]), "tok", axis=0)
    piece_ids = meta[:, 0, :]
    piece_live = meta[:, 1, :] == 1
    vocab_ids = tok_place * slice_width + jnp.arange(slice_width, dtype=jnp.int32)
    flat_stats = slice_stats(gathered, piece_ids.reshape(-1), head_weight, vocab_ids)
    top_p, total_p, moment_p, chosen_p = (part.reshape(tok_count, local_rows) for part in flat_stats)

    seq_ends = jnp.cumsum(lengths)
    seq_ids = jnp.arange(seq_count, dtype=jnp.int32)
    block_of = jnp.arange(tok_count, dtype=jnp.int32) * rep_count + rep_place
    piece_rows = block_of[:, None] * local_rows + jnp.arange(local_rows, dtype=jnp.int32)[None, :]
    piece_seq = jnp.sum((seq_ends[None, None, :] <= piece_rows[:, :, None]).astype(jnp.int32), axis=2)
    member = (piece_seq[:, :, None] == seq_ids[None, None, :]) & piece_live[:, :, None]
    part_max = jnp.max(jnp.where(member, top_p[:, :, None], NEG_FILL), axis=(0, 1))
    device_place = tok_place * rep_count + rep_place
    own_rows = device_place * local_rows + jnp.arange(local_rows, dtype=jnp.int32)
    part_norm = jnp.sum(
        jnp.where(own_rows[:, None] == seq_ends[None, :] - 1, state_norm[:, None], 0.0), axis=0
    )

    earlier_same = (owner_map[None, :] == owner_map[:, None]) & (seq_ids[None, :] < seq_ids[:, None])
    slot_rank = jnp.sum(earlier_same.astype(jnp.int32), axis=1)
    device_ids = jnp.arange(tok_count * rep_count, dtype=jnp.int32)
    slot_hot = (owner_map[:, None, None] == device_ids[None, :, None]) & (
        slot_rank[:, None, None] == jnp.arange(SLOTS, dtype=jnp.int32)[None, None, :]
    )
    req_max = jnp.max(jnp.where(slot_hot, part_max[:, None, None], NEG_FILL), axis=0)
    req_norm = jnp.sum(jnp.where(slot_hot, part_norm[:, None, None], 0.0), axis=0)
    req = jnp.stack([req_max, req_norm], axis=2).reshape(tok_count, rep_count * SLOTS * 2)

    stats = jnp.stack([top_p, total_p, moment_p, chosen_p], axis=2).reshape(tok_count, local_rows * 4)
    outgoing = jnp.concatenate([stats, req], axis=1)
    incoming = lax.all_to_all(outgoing, "tok", 0, 0, tiled=True)

    in_stats = incoming[:, : local_rows * 4].reshape(tok_count, local_rows, 4)
    tops = in_stats[:, :, 0]
    row_top = jnp.max(tops, axis=0)
    scale = jnp.exp(tops - row_top[None, :])
    row_total = jnp.sum(in_stats[:, :, 1] * scale, axis=0)
    row_moment = jnp.sum(in_stats[:, :, 2] * scale, axis=0)
    row_chosen = jnp.sum(in_stats[:, :, 3], axis=0)
    log_total = jnp.log(row_total)
    logprob = jnp.where(live_row, row_chosen - row_top - log_total, 0.0)
    entropy = jnp.where(live_row, row_top + log_total - row_moment / row_total, 0.0)

    in_req = incoming[:, local_rows * 4:].reshape(tok_count, rep_count, SLOTS, 2)
    rep_max = jnp.max(in_req[..., 0], axis=0)
    rep_norm = jnp.sum(in_req[..., 1], axis=0)
    rep_pair = jnp.stack([rep_max, rep_norm], axis=2)
    got = lax.all_to_all(rep_pair, "rep", 0, 0, tiled=True)
    final_max = jnp.max(got[..., 0], axis=0)
    final_norm = jnp.sum(got[..., 1], axis=0)
    has_slot = jnp.any(slot_hot[:, device_place, :], axis=0)
    request_table = jnp.where(
        has_slot[:, None], jnp.stack([final_max, final_norm], axis=1), 0.0
    )
    return (logprob, entropy, request_table[None])


def solution(mesh):
    return jax.shard_map(
        shards,
        mesh=mesh,
        in_specs=(
            P(("tok", "rep"), None),
            P(),
            P("tok", None),
            P(("tok", "rep")),
            P(),
            P(("tok", "rep")),
            P(),
        ),
        out_specs=(P(("tok", "rep")), P(("tok", "rep")), P(("tok", "rep"), None, None)),
        check_vma=False,
    )
```

```python
import jax
import jax.numpy as jnp
from jax import lax
from jax.experimental import pallas as pl
from jax.experimental.pallas import tpu as pltpu
from jax.sharding import PartitionSpec as P

SLOTS = 2


EPSILON = 1e-06
NEG_FILL = -1e30


TILE = 512
VOCAB_PAD = 256


def stats_kernel(head_ref, vocab_ref, ids_ref, rows_ref, out_ref):
    logits = lax.dot_general(
        head_ref[...], rows_ref[...], (((1,), (1,)), ((), ())), preferred_element_type=jnp.float32
    )
    real = vocab_ref[...] >= 0
    logits = jnp.where(real, logits, -jnp.inf)
    row_top = jnp.max(logits, axis=0, keepdims=True)
    weights = jnp.where(real, jnp.exp(logits - row_top), 0.0)
    row_total = jnp.sum(weights, axis=0, keepdims=True)
    moment = jnp.sum(jnp.where(real, weights * logits, 0.0), axis=0, keepdims=True)
    chosen = jnp.sum(jnp.where(vocab_ref[...] == ids_ref[...], logits, 0.0), axis=0, keepdims=True)
    out_ref[...] = jnp.concatenate(
        [row_top, row_total, moment, chosen, jnp.zeros((4, row_top.shape[1]), jnp.float32)], axis=0
    )


def slice_stats(rows, ids, head_weight, vocab_ids):
    count, width = rows.shape
    tile = TILE if count % TILE == 0 else count
    slice_width = head_weight.shape[0]
    head = jnp.concatenate(
        [head_weight, jnp.zeros((VOCAB_PAD - slice_width, width), head_weight.dtype)], axis=0
    )
    vocab = jnp.concatenate(
        [vocab_ids, jnp.full((VOCAB_PAD - slice_width,), -1, jnp.int32)]
    )[:, None]
    out = pl.pallas_call(
        stats_kernel,
        grid=(count // tile,),
        in_specs=[
            pl.BlockSpec((VOCAB_PAD, width), lambda i: (0, 0)),
            pl.BlockSpec((VOCAB_PAD, 1), lambda i: (0, 0)),
            pl.BlockSpec((1, tile), lambda i: (0, i)),
            pl.BlockSpec((tile, width), lambda i: (i, 0)),
        ],
        out_specs=pl.BlockSpec((8, tile), lambda i: (0, i)),
        out_shape=jax.ShapeDtypeStruct((8, count), jnp.float32),
        cost_estimate=pl.CostEstimate(
            flops=2 * VOCAB_PAD * width * count,
            transcendentals=VOCAB_PAD * count,
            bytes_accessed=count * width * 2 + VOCAB_PAD * width * 2 + count * 36,
        ),
    )(head, vocab, ids[None, :], rows)
    return out[0], out[1], out[2], out[3]


def shards(hidden, norm_gain, head_weight, targets, lengths, padding_mask, owner_map):
    tok_count = lax.axis_size("tok")
    rep_count = lax.axis_size("rep")
    tok_place = lax.axis_index("tok")
    rep_place = lax.axis_index("rep")
    local_rows, width = hidden.shape
    slice_width = head_weight.shape[0]
    seq_count = lengths.shape[0]

    widened = hidden.astype(jnp.float32)
    mean_square = jnp.mean(widened * widened, axis=1)
    normed = (
        widened * lax.rsqrt(mean_square + EPSILON)[:, None] * norm_gain.astype(jnp.float32)[None, :]
    ).astype(jnp.bfloat16)
    state_norm = jnp.sqrt(mean_square)
    live_row = padding_mask == 1

    gathered = lax.all_gather(normed, "tok", axis=0, tiled=True)
    meta = lax.all_gather(jnp.stack([targets, padding_mask]), "tok", axis=0)
    piece_ids = meta[:, 0, :]
    piece_live = meta[:, 1, :] == 1
    vocab_ids = tok_place * slice_width + jnp.arange(slice_width, dtype=jnp.int32)
    flat_stats = slice_stats(gathered, piece_ids.reshape(-1), head_weight, vocab_ids)
    top_p, total_p, moment_p, chosen_p = (part.reshape(tok_count, local_rows) for part in flat_stats)

    seq_ends = jnp.cumsum(lengths)
    seq_ids = jnp.arange(seq_count, dtype=jnp.int32)
    block_of = jnp.arange(tok_count, dtype=jnp.int32) * rep_count + rep_place
    piece_rows = block_of[:, None] * local_rows + jnp.arange(local_rows, dtype=jnp.int32)[None, :]
    piece_seq = jnp.sum((seq_ends[None, None, :] <= piece_rows[:, :, None]).astype(jnp.int32), axis=2)
    member = (piece_seq[:, :, None] == seq_ids[None, None, :]) & piece_live[:, :, None]
    part_max = jnp.max(jnp.where(member, top_p[:, :, None], NEG_FILL), axis=(0, 1))
    device_place = tok_place * rep_count + rep_place
    own_rows = device_place * local_rows + jnp.arange(local_rows, dtype=jnp.int32)
    part_norm = jnp.sum(
        jnp.where(own_rows[:, None] == seq_ends[None, :] - 1, state_norm[:, None], 0.0), axis=0
    )

    earlier_same = (owner_map[None, :] == owner_map[:, None]) & (seq_ids[None, :] < seq_ids[:, None])
    slot_rank = jnp.sum(earlier_same.astype(jnp.int32), axis=1)
    device_ids = jnp.arange(tok_count * rep_count, dtype=jnp.int32)
    slot_hot = (owner_map[:, None, None] == device_ids[None, :, None]) & (
        slot_rank[:, None, None] == jnp.arange(SLOTS, dtype=jnp.int32)[None, None, :]
    )
    req_max = jnp.max(jnp.where(slot_hot, part_max[:, None, None], NEG_FILL), axis=0)
    req_norm = jnp.sum(jnp.where(slot_hot, part_norm[:, None, None], 0.0), axis=0)
    req = jnp.stack([req_max, req_norm], axis=2).reshape(tok_count * rep_count, SLOTS * 2)

    stats = jnp.stack([top_p, total_p, moment_p, chosen_p], axis=2).reshape(tok_count, local_rows * 4)
    same_rep = jnp.arange(rep_count, dtype=jnp.int32)[None, :, None] == rep_place
    spread = jnp.where(same_rep, stats[:, None, :], 0.0).reshape(tok_count * rep_count, local_rows * 4)
    outgoing = jnp.concatenate([spread, req], axis=1)
    incoming = lax.all_to_all(outgoing, ("tok", "rep"), 0, 0, tiled=True)

    by_rep = incoming[:, : local_rows * 4].reshape(tok_count, rep_count, local_rows * 4)
    in_stats = lax.dynamic_index_in_dim(by_rep, rep_place, 1, keepdims=False).reshape(tok_count, local_rows, 4)
    tops = in_stats[:, :, 0]
    row_top = jnp.max(tops, axis=0)
    scale = jnp.exp(tops - row_top[None, :])
    row_total = jnp.sum(in_stats[:, :, 1] * scale, axis=0)
    row_moment = jnp.sum(in_stats[:, :, 2] * scale, axis=0)
    row_chosen = jnp.sum(in_stats[:, :, 3], axis=0)
    log_total = jnp.log(row_total)
    logprob = jnp.where(live_row, row_chosen - row_top - log_total, 0.0)
    entropy = jnp.where(live_row, row_top + log_total - row_moment / row_total, 0.0)

    in_req = incoming[:, local_rows * 4:].reshape(tok_count * rep_count, SLOTS, 2)
    final_max = jnp.max(in_req[..., 0], axis=0)
    final_norm = jnp.sum(in_req[..., 1], axis=0)
    has_slot = jnp.any(slot_hot[:, device_place, :], axis=0)
    request_table = jnp.where(
        has_slot[:, None], jnp.stack([final_max, final_norm], axis=1), 0.0
    )
    return (logprob, entropy, request_table[None])


def solution(mesh):
    return jax.shard_map(
        shards,
        mesh=mesh,
        in_specs=(
            P(("tok", "rep"), None),
            P(),
            P("tok", None),
            P(("tok", "rep")),
            P(),
            P(("tok", "rep")),
            P(),
        ),
        out_specs=(P(("tok", "rep")), P(("tok", "rep")), P(("tok", "rep"), None, None)),
        check_vma=False,
    )
```

```python
import jax
import jax.numpy as jnp
from jax import lax
from jax.experimental import pallas as pl
from jax.experimental.pallas import tpu as pltpu
from jax.sharding import PartitionSpec as P

SLOTS = 2


EPSILON = 1e-06
NEG_FILL = -1e30


TILE = 1024
VOCAB_PAD = 256


def stats_kernel(head_ref, vocab_ref, ids_ref, rows_ref, out_ref):
    logits = lax.dot_general(
        head_ref[...], rows_ref[...], (((1,), (1,)), ((), ())), preferred_element_type=jnp.float32
    )
    real = vocab_ref[...] >= 0
    logits = jnp.where(real, logits, -jnp.inf)
    row_top = jnp.max(logits, axis=0, keepdims=True)
    weights = jnp.where(real, jnp.exp(logits - row_top), 0.0)
    row_total = jnp.sum(weights, axis=0, keepdims=True)
    moment = jnp.sum(jnp.where(real, weights * logits, 0.0), axis=0, keepdims=True)
    chosen = jnp.sum(jnp.where(vocab_ref[...] == ids_ref[...], logits, 0.0), axis=0, keepdims=True)
    out_ref[...] = jnp.concatenate(
        [row_top, row_total, moment, chosen, jnp.zeros((4, row_top.shape[1]), jnp.float32)], axis=0
    )


def slice_stats(rows, ids, head_weight, vocab_ids):
    count, width = rows.shape
    tile = TILE if count % TILE == 0 else count
    slice_width = head_weight.shape[0]
    head = jnp.concatenate(
        [head_weight, jnp.zeros((VOCAB_PAD - slice_width, width), head_weight.dtype)], axis=0
    )
    vocab = jnp.concatenate(
        [vocab_ids, jnp.full((VOCAB_PAD - slice_width,), -1, jnp.int32)]
    )[:, None]
    out = pl.pallas_call(
        stats_kernel,
        grid=(count // tile,),
        in_specs=[
            pl.BlockSpec((VOCAB_PAD, width), lambda i: (0, 0)),
            pl.BlockSpec((VOCAB_PAD, 1), lambda i: (0, 0)),
            pl.BlockSpec((1, tile), lambda i: (0, i)),
            pl.BlockSpec((tile, width), lambda i: (i, 0)),
        ],
        out_specs=pl.BlockSpec((8, tile), lambda i: (0, i)),
        out_shape=jax.ShapeDtypeStruct((8, count), jnp.float32),
        cost_estimate=pl.CostEstimate(
            flops=2 * VOCAB_PAD * width * count,
            transcendentals=VOCAB_PAD * count,
            bytes_accessed=count * width * 2 + VOCAB_PAD * width * 2 + count * 36,
        ),
    )(head, vocab, ids[None, :], rows)
    return out[0], out[1], out[2], out[3]


def norm_kernel(hidden_ref, gain_ref, normed_ref, square_ref):
    widened = hidden_ref[...].astype(jnp.float32)
    mean_square = jnp.mean(widened * widened, axis=1, keepdims=True)
    normed_ref[...] = (
        widened * lax.rsqrt(mean_square + EPSILON) * gain_ref[...].astype(jnp.float32)
    ).astype(normed_ref.dtype)
    square_ref[...] = jnp.broadcast_to(mean_square, square_ref.shape)


def rms_norm(hidden, norm_gain):
    rows, width = hidden.shape
    normed, square = pl.pallas_call(
        norm_kernel,
        out_shape=(
            jax.ShapeDtypeStruct((rows, width), jnp.bfloat16),
            jax.ShapeDtypeStruct((rows, 128), jnp.float32),
        ),
    )(hidden, norm_gain[None, :])
    return normed, square[:, 0]


def shards(hidden, norm_gain, head_weight, targets, lengths, padding_mask, owner_map):
    tok_count = lax.axis_size("tok")
    rep_count = lax.axis_size("rep")
    tok_place = lax.axis_index("tok")
    rep_place = lax.axis_index("rep")
    local_rows, width = hidden.shape
    slice_width = head_weight.shape[0]
    seq_count = lengths.shape[0]

    normed, mean_square = rms_norm(hidden, norm_gain)
    state_norm = jnp.sqrt(mean_square)
    live_row = padding_mask == 1

    gathered = lax.all_gather(normed, "tok", axis=0, tiled=True)
    meta = lax.all_gather(jnp.stack([targets, padding_mask]), "tok", axis=0)
    piece_ids = meta[:, 0, :]
    piece_live = meta[:, 1, :] == 1
    vocab_ids = tok_place * slice_width + jnp.arange(slice_width, dtype=jnp.int32)
    flat_stats = slice_stats(gathered, piece_ids.reshape(-1), head_weight, vocab_ids)
    top_p, total_p, moment_p, chosen_p = (part.reshape(tok_count, local_rows) for part in flat_stats)

    seq_ends = jnp.cumsum(lengths)
    seq_ids = jnp.arange(seq_count, dtype=jnp.int32)
    block_of = jnp.arange(tok_count, dtype=jnp.int32) * rep_count + rep_place
    piece_rows = block_of[:, None] * local_rows + jnp.arange(local_rows, dtype=jnp.int32)[None, :]
    piece_seq = jnp.sum((seq_ends[None, None, :] <= piece_rows[:, :, None]).astype(jnp.int32), axis=2)
    member = (piece_seq[:, :, None] == seq_ids[None, None, :]) & piece_live[:, :, None]
    part_max = jnp.max(jnp.where(member, top_p[:, :, None], NEG_FILL), axis=(0, 1))
    device_place = tok_place * rep_count + rep_place
    own_rows = device_place * local_rows + jnp.arange(local_rows, dtype=jnp.int32)
    part_norm = jnp.sum(
        jnp.where(own_rows[:, None] == seq_ends[None, :] - 1, state_norm[:, None], 0.0), axis=0
    )

    earlier_same = (owner_map[None, :] == owner_map[:, None]) & (seq_ids[None, :] < seq_ids[:, None])
    slot_rank = jnp.sum(earlier_same.astype(jnp.int32), axis=1)
    device_ids = jnp.arange(tok_count * rep_count, dtype=jnp.int32)
    slot_hot = (owner_map[:, None, None] == device_ids[None, :, None]) & (
        slot_rank[:, None, None] == jnp.arange(SLOTS, dtype=jnp.int32)[None, None, :]
    )
    req_max = jnp.max(jnp.where(slot_hot, part_max[:, None, None], NEG_FILL), axis=0)
    req_norm = jnp.sum(jnp.where(slot_hot, part_norm[:, None, None], 0.0), axis=0)
    req = jnp.stack([req_max, req_norm], axis=2).reshape(tok_count, rep_count * SLOTS * 2)

    stats = jnp.stack([top_p, total_p, moment_p, chosen_p], axis=2).reshape(tok_count, local_rows * 4)
    outgoing = jnp.concatenate([stats, req], axis=1)
    incoming = lax.all_to_all(outgoing, "tok", 0, 0, tiled=True)

    in_stats = incoming[:, : local_rows * 4].reshape(tok_count, local_rows, 4)
    tops = in_stats[:, :, 0]
    row_top = jnp.max(tops, axis=0)
    scale = jnp.exp(tops - row_top[None, :])
    row_total = jnp.sum(in_stats[:, :, 1] * scale, axis=0)
    row_moment = jnp.sum(in_stats[:, :, 2] * scale, axis=0)
    row_chosen = jnp.sum(in_stats[:, :, 3], axis=0)
    log_total = jnp.log(row_total)
    logprob = jnp.where(live_row, row_chosen - row_top - log_total, 0.0)
    entropy = jnp.where(live_row, row_top + log_total - row_moment / row_total, 0.0)

    in_req = incoming[:, local_rows * 4:].reshape(tok_count, rep_count, SLOTS, 2)
    rep_max = jnp.max(in_req[..., 0], axis=0)
    rep_norm = jnp.sum(in_req[..., 1], axis=0)
    rep_pair = jnp.stack([rep_max, rep_norm], axis=2)
    got = lax.all_to_all(rep_pair, "rep", 0, 0, tiled=True)
    final_max = jnp.max(got[..., 0], axis=0)
    final_norm = jnp.sum(got[..., 1], axis=0)
    has_slot = jnp.any(slot_hot[:, device_place, :], axis=0)
    request_table = jnp.where(
        has_slot[:, None], jnp.stack([final_max, final_norm], axis=1), 0.0
    )
    return (logprob, entropy, request_table[None])


def solution(mesh):
    return jax.shard_map(
        shards,
        mesh=mesh,
        in_specs=(
            P(("tok", "rep"), None),
            P(),
            P("tok", None),
            P(("tok", "rep")),
            P(),
            P(("tok", "rep")),
            P(),
        ),
        out_specs=(P(("tok", "rep")), P(("tok", "rep")), P(("tok", "rep"), None, None)),
        check_vma=False,
    )
```

```python
import jax
import jax.numpy as jnp
from jax import lax
from jax.experimental import pallas as pl
from jax.experimental.pallas import tpu as pltpu
from jax.sharding import PartitionSpec as P

SLOTS = 2


EPSILON = 1e-06
NEG_FILL = -1e30


TILE = 1024
VOCAB_PAD = 256


def stats_kernel(head_ref, vocab_ref, ids_ref, rows_ref, out_ref):
    logits = lax.dot_general(
        head_ref[...], rows_ref[...], (((1,), (1,)), ((), ())), preferred_element_type=jnp.float32
    )
    real = vocab_ref[...] >= 0
    logits = jnp.where(real, logits, -jnp.inf)
    row_top = jnp.max(logits, axis=0, keepdims=True)
    weights = jnp.where(real, jnp.exp(logits - row_top), 0.0)
    row_total = jnp.sum(weights, axis=0, keepdims=True)
    moment = jnp.sum(jnp.where(real, weights * logits, 0.0), axis=0, keepdims=True)
    chosen = jnp.sum(jnp.where(vocab_ref[...] == ids_ref[...], logits, 0.0), axis=0, keepdims=True)
    out_ref[...] = jnp.concatenate(
        [row_top, row_total, moment, chosen, jnp.zeros((4, row_top.shape[1]), jnp.float32)], axis=0
    )


def slice_stats(rows, ids, head_weight, vocab_ids):
    count, width = rows.shape
    tile = TILE if count % TILE == 0 else count
    slice_width = head_weight.shape[0]
    head = jnp.concatenate(
        [head_weight, jnp.zeros((VOCAB_PAD - slice_width, width), head_weight.dtype)], axis=0
    )
    vocab = jnp.concatenate(
        [vocab_ids, jnp.full((VOCAB_PAD - slice_width,), -1, jnp.int32)]
    )[:, None]
    out = pl.pallas_call(
        stats_kernel,
        grid=(count // tile,),
        in_specs=[
            pl.BlockSpec((VOCAB_PAD, width), lambda i: (0, 0)),
            pl.BlockSpec((VOCAB_PAD, 1), lambda i: (0, 0)),
            pl.BlockSpec((1, tile), lambda i: (0, i)),
            pl.BlockSpec((tile, width), lambda i: (i, 0)),
        ],
        out_specs=pl.BlockSpec((8, tile), lambda i: (0, i)),
        out_shape=jax.ShapeDtypeStruct((8, count), jnp.float32),
        cost_estimate=pl.CostEstimate(
            flops=2 * VOCAB_PAD * width * count,
            transcendentals=VOCAB_PAD * count,
            bytes_accessed=count * width * 2 + VOCAB_PAD * width * 2 + count * 36,
        ),
    )(head, vocab, ids[None, :], rows)
    return out[0], out[1], out[2], out[3]


def norm_kernel(hidden_ref, gain_ref, normed_ref, square_ref):
    widened = hidden_ref[...].astype(jnp.float32)
    mean_square = jnp.mean(widened * widened, axis=1, keepdims=True)
    normed_ref[...] = (
        widened * lax.rsqrt(mean_square + EPSILON) * gain_ref[...].astype(jnp.float32)[None, :]
    ).astype(normed_ref.dtype)
    square_ref[...] = jnp.broadcast_to(mean_square, square_ref.shape)


def rms_norm(hidden, norm_gain):
    rows, width = hidden.shape
    normed, square = pl.pallas_call(
        norm_kernel,
        out_shape=(
            jax.ShapeDtypeStruct((rows, width), jnp.bfloat16),
            jax.ShapeDtypeStruct((rows, 128), jnp.float32),
        ),
    )(hidden, norm_gain)
    return normed, square[:, 0]


def shards(hidden, norm_gain, head_weight, targets, lengths, padding_mask, owner_map):
    tok_count = lax.axis_size("tok")
    rep_count = lax.axis_size("rep")
    tok_place = lax.axis_index("tok")
    rep_place = lax.axis_index("rep")
    local_rows, width = hidden.shape
    slice_width = head_weight.shape[0]
    seq_count = lengths.shape[0]

    normed, mean_square = rms_norm(hidden, norm_gain)
    state_norm = jnp.sqrt(mean_square)
    live_row = padding_mask == 1

    gathered = lax.all_gather(normed, "tok", axis=0, tiled=True)
    meta = lax.all_gather(jnp.stack([targets, padding_mask]), "tok", axis=0)
    piece_ids = meta[:, 0, :]
    piece_live = meta[:, 1, :] == 1
    vocab_ids = tok_place * slice_width + jnp.arange(slice_width, dtype=jnp.int32)
    flat_stats = slice_stats(gathered, piece_ids.reshape(-1), head_weight, vocab_ids)
    top_p, total_p, moment_p, chosen_p = (part.reshape(tok_count, local_rows) for part in flat_stats)

    seq_ends = jnp.cumsum(lengths)
    seq_ids = jnp.arange(seq_count, dtype=jnp.int32)
    block_of = jnp.arange(tok_count, dtype=jnp.int32) * rep_count + rep_place
    piece_rows = block_of[:, None] * local_rows + jnp.arange(local_rows, dtype=jnp.int32)[None, :]
    piece_seq = jnp.sum((seq_ends[None, None, :] <= piece_rows[:, :, None]).astype(jnp.int32), axis=2)
    member = (piece_seq[:, :, None] == seq_ids[None, None, :]) & piece_live[:, :, None]
    part_max = jnp.max(jnp.where(member, top_p[:, :, None], NEG_FILL), axis=(0, 1))
    device_place = tok_place * rep_count + rep_place
    own_rows = device_place * local_rows + jnp.arange(local_rows, dtype=jnp.int32)
    part_norm = jnp.sum(
        jnp.where(own_rows[:, None] == seq_ends[None, :] - 1, state_norm[:, None], 0.0), axis=0
    )

    earlier_same = (owner_map[None, :] == owner_map[:, None]) & (seq_ids[None, :] < seq_ids[:, None])
    slot_rank = jnp.sum(earlier_same.astype(jnp.int32), axis=1)
    device_ids = jnp.arange(tok_count * rep_count, dtype=jnp.int32)
    slot_hot = (owner_map[:, None, None] == device_ids[None, :, None]) & (
        slot_rank[:, None, None] == jnp.arange(SLOTS, dtype=jnp.int32)[None, None, :]
    )
    req_max = jnp.max(jnp.where(slot_hot, part_max[:, None, None], NEG_FILL), axis=0)
    req_norm = jnp.sum(jnp.where(slot_hot, part_norm[:, None, None], 0.0), axis=0)
    req = jnp.stack([req_max, req_norm], axis=2).reshape(tok_count, rep_count * SLOTS * 2)

    stats = jnp.stack([top_p, total_p, moment_p, chosen_p], axis=2).reshape(tok_count, local_rows * 4)
    outgoing = jnp.concatenate([stats, req], axis=1)
    incoming = lax.all_to_all(outgoing, "tok", 0, 0, tiled=True)

    in_stats = incoming[:, : local_rows * 4].reshape(tok_count, local_rows, 4)
    tops = in_stats[:, :, 0]
    row_top = jnp.max(tops, axis=0)
    scale = jnp.exp(tops - row_top[None, :])
    row_total = jnp.sum(in_stats[:, :, 1] * scale, axis=0)
    row_moment = jnp.sum(in_stats[:, :, 2] * scale, axis=0)
    row_chosen = jnp.sum(in_stats[:, :, 3], axis=0)
    log_total = jnp.log(row_total)
    logprob = jnp.where(live_row, row_chosen - row_top - log_total, 0.0)
    entropy = jnp.where(live_row, row_top + log_total - row_moment / row_total, 0.0)

    in_req = incoming[:, local_rows * 4:].reshape(tok_count, rep_count, SLOTS, 2)
    rep_max = jnp.max(in_req[..., 0], axis=0)
    rep_norm = jnp.sum(in_req[..., 1], axis=0)
    rep_pair = jnp.stack([rep_max, rep_norm], axis=2)
    got = lax.all_to_all(rep_pair, "rep", 0, 0, tiled=True)
    final_max = jnp.max(got[..., 0], axis=0)
    final_norm = jnp.sum(got[..., 1], axis=0)
    has_slot = jnp.any(slot_hot[:, device_place, :], axis=0)
    request_table = jnp.where(
        has_slot[:, None], jnp.stack([final_max, final_norm], axis=1), 0.0
    )
    return (logprob, entropy, request_table[None])


def solution(mesh):
    return jax.shard_map(
        shards,
        mesh=mesh,
        in_specs=(
            P(("tok", "rep"), None),
            P(),
            P("tok", None),
            P(("tok", "rep")),
            P(),
            P(("tok", "rep")),
            P(),
        ),
        out_specs=(P(("tok", "rep")), P(("tok", "rep")), P(("tok", "rep"), None, None)),
        check_vma=False,
    )
```

```python
import jax
import jax.numpy as jnp
from jax import lax
from jax.experimental import pallas as pl
from jax.experimental.pallas import tpu as pltpu
from jax.sharding import PartitionSpec as P

SLOTS = 2


EPSILON = 1e-06
NEG_FILL = -1e30


TILE = 1536
VOCAB_PAD = 256


def stats_kernel(head_ref, vocab_ref, ids_ref, rows_ref, out_ref):
    logits = lax.dot_general(
        head_ref[...], rows_ref[...], (((1,), (1,)), ((), ())), preferred_element_type=jnp.float32
    )
    logits = jnp.where(vocab_ref[...] >= 0, logits, NEG_FILL)
    row_top = jnp.max(logits, axis=0, keepdims=True)
    weights = jnp.exp(logits - row_top)
    row_total = jnp.sum(weights, axis=0, keepdims=True)
    moment = jnp.sum(weights * logits, axis=0, keepdims=True)
    chosen = jnp.sum(jnp.where(vocab_ref[...] == ids_ref[...], logits, 0.0), axis=0, keepdims=True)
    out_ref[...] = jnp.concatenate(
        [row_top, row_total, moment, chosen, jnp.zeros((4, row_top.shape[1]), jnp.float32)], axis=0
    )


def slice_stats(rows, ids, head_weight, vocab_ids):
    count, width = rows.shape
    tile = TILE if count % TILE == 0 else count
    slice_width = head_weight.shape[0]
    head = jnp.concatenate(
        [head_weight, jnp.zeros((VOCAB_PAD - slice_width, width), head_weight.dtype)], axis=0
    )
    vocab = jnp.concatenate(
        [vocab_ids, jnp.full((VOCAB_PAD - slice_width,), -1, jnp.int32)]
    )[:, None]
    out = pl.pallas_call(
        stats_kernel,
        grid=(count // tile,),
        in_specs=[
            pl.BlockSpec((VOCAB_PAD, width), lambda i: (0, 0)),
            pl.BlockSpec((VOCAB_PAD, 1), lambda i: (0, 0)),
            pl.BlockSpec((1, tile), lambda i: (0, i)),
            pl.BlockSpec((tile, width), lambda i: (i, 0)),
        ],
        out_specs=pl.BlockSpec((8, tile), lambda i: (0, i)),
        out_shape=jax.ShapeDtypeStruct((8, count), jnp.float32),
        cost_estimate=pl.CostEstimate(
            flops=2 * VOCAB_PAD * width * count,
            transcendentals=VOCAB_PAD * count,
            bytes_accessed=count * width * 2 + VOCAB_PAD * width * 2 + count * 36,
        ),
    )(head, vocab, ids[None, :], rows)
    return out[0], out[1], out[2], out[3]


def norm_kernel(hidden_ref, gain_ref, normed_ref, square_ref):
    widened = hidden_ref[...].astype(jnp.float32)
    mean_square = jnp.mean(widened * widened, axis=1, keepdims=True)
    normed_ref[...] = (
        widened * lax.rsqrt(mean_square + EPSILON) * gain_ref[...].astype(jnp.float32)
    ).astype(normed_ref.dtype)
    square_ref[...] = jnp.broadcast_to(mean_square, square_ref.shape)


def rms_norm(hidden, norm_gain):
    rows, width = hidden.shape
    normed, square = pl.pallas_call(
        norm_kernel,
        out_shape=(
            jax.ShapeDtypeStruct((rows, width), jnp.bfloat16),
            jax.ShapeDtypeStruct((rows, 128), jnp.float32),
        ),
    )(hidden, norm_gain[None, :])
    return normed, square[:, 0]


def shards(hidden, norm_gain, head_weight, targets, lengths, padding_mask, owner_map):
    tok_count = lax.axis_size("tok")
    rep_count = lax.axis_size("rep")
    tok_place = lax.axis_index("tok")
    rep_place = lax.axis_index("rep")
    local_rows, width = hidden.shape
    slice_width = head_weight.shape[0]
    seq_count = lengths.shape[0]

    normed, mean_square = rms_norm(hidden, norm_gain)
    state_norm = jnp.sqrt(mean_square)
    live_row = padding_mask == 1

    gathered = lax.all_gather(normed, "tok", axis=0, tiled=True)
    meta = lax.all_gather(jnp.stack([targets, padding_mask]), "tok", axis=0)
    piece_ids = meta[:, 0, :]
    piece_live = meta[:, 1, :] == 1
    vocab_ids = tok_place * slice_width + jnp.arange(slice_width, dtype=jnp.int32)
    flat_stats = slice_stats(gathered, piece_ids.reshape(-1), head_weight, vocab_ids)
    top_p, total_p, moment_p, chosen_p = (part.reshape(tok_count, local_rows) for part in flat_stats)

    seq_ends = jnp.cumsum(lengths)
    seq_ids = jnp.arange(seq_count, dtype=jnp.int32)
    block_of = jnp.arange(tok_count, dtype=jnp.int32) * rep_count + rep_place
    piece_rows = block_of[:, None] * local_rows + jnp.arange(local_rows, dtype=jnp.int32)[None, :]
    piece_seq = jnp.sum((seq_ends[None, None, :] <= piece_rows[:, :, None]).astype(jnp.int32), axis=2)
    member = (piece_seq[:, :, None] == seq_ids[None, None, :]) & piece_live[:, :, None]
    part_max = jnp.max(jnp.where(member, top_p[:, :, None], NEG_FILL), axis=(0, 1))
    device_place = tok_place * rep_count + rep_place
    own_rows = device_place * local_rows + jnp.arange(local_rows, dtype=jnp.int32)
    part_norm = jnp.sum(
        jnp.where(own_rows[:, None] == seq_ends[None, :] - 1, state_norm[:, None], 0.0), axis=0
    )

    earlier_same = (owner_map[None, :] == owner_map[:, None]) & (seq_ids[None, :] < seq_ids[:, None])
    slot_rank = jnp.sum(earlier_same.astype(jnp.int32), axis=1)
    device_ids = jnp.arange(tok_count * rep_count, dtype=jnp.int32)
    slot_hot = (owner_map[:, None, None] == device_ids[None, :, None]) & (
        slot_rank[:, None, None] == jnp.arange(SLOTS, dtype=jnp.int32)[None, None, :]
    )
    req_max = jnp.max(jnp.where(slot_hot, part_max[:, None, None], NEG_FILL), axis=0)
    req_norm = jnp.sum(jnp.where(slot_hot, part_norm[:, None, None], 0.0), axis=0)
    req = jnp.stack([req_max, req_norm], axis=2).reshape(tok_count, rep_count * SLOTS * 2)

    stats = jnp.stack([top_p, total_p, moment_p, chosen_p], axis=2).reshape(tok_count, local_rows * 4)
    outgoing = jnp.concatenate([stats, req], axis=1)
    incoming = lax.all_to_all(outgoing, "tok", 0, 0, tiled=True)

    in_stats = incoming[:, : local_rows * 4].reshape(tok_count, local_rows, 4)
    tops = in_stats[:, :, 0]
    row_top = jnp.max(tops, axis=0)
    scale = jnp.exp(tops - row_top[None, :])
    row_total = jnp.sum(in_stats[:, :, 1] * scale, axis=0)
    row_moment = jnp.sum(in_stats[:, :, 2] * scale, axis=0)
    row_chosen = jnp.sum(in_stats[:, :, 3], axis=0)
    log_total = jnp.log(row_total)
    logprob = jnp.where(live_row, row_chosen - row_top - log_total, 0.0)
    entropy = jnp.where(live_row, row_top + log_total - row_moment / row_total, 0.0)

    in_req = incoming[:, local_rows * 4:].reshape(tok_count, rep_count, SLOTS, 2)
    rep_max = jnp.max(in_req[..., 0], axis=0)
    rep_norm = jnp.sum(in_req[..., 1], axis=0)
    rep_pair = jnp.stack([rep_max, rep_norm], axis=2)
    got = lax.all_to_all(rep_pair, "rep", 0, 0, tiled=True)
    final_max = jnp.max(got[..., 0], axis=0)
    final_norm = jnp.sum(got[..., 1], axis=0)
    has_slot = jnp.any(slot_hot[:, device_place, :], axis=0)
    request_table = jnp.where(
        has_slot[:, None], jnp.stack([final_max, final_norm], axis=1), 0.0
    )
    return (logprob, entropy, request_table[None])


def solution(mesh):
    return jax.shard_map(
        shards,
        mesh=mesh,
        in_specs=(
            P(("tok", "rep"), None),
            P(),
            P("tok", None),
            P(("tok", "rep")),
            P(),
            P(("tok", "rep")),
            P(),
        ),
        out_specs=(P(("tok", "rep")), P(("tok", "rep")), P(("tok", "rep"), None, None)),
        check_vma=False,
    )
```

```python
import jax
import jax.numpy as jnp
from jax import lax
from jax.experimental import pallas as pl
from jax.experimental.pallas import tpu as pltpu
from jax.sharding import PartitionSpec as P

SLOTS = 2


EPSILON = 1e-06
NEG_FILL = -1e30


TILE = 1536
VOCAB_PAD = 256


def stats_kernel(head_ref, vocab_ref, ids_ref, rows_ref, out_ref):
    logits = lax.dot_general(
        head_ref[...], rows_ref[...], (((1,), (1,)), ((), ())), preferred_element_type=jnp.float32
    )
    logits = jnp.where(vocab_ref[...] >= 0, logits, NEG_FILL)
    row_top = jnp.max(logits, axis=0, keepdims=True)
    weights = jnp.exp(logits - row_top)
    row_total = jnp.sum(weights, axis=0, keepdims=True)
    moment = jnp.sum(weights * logits, axis=0, keepdims=True)
    chosen = jnp.sum(jnp.where(vocab_ref[...] == ids_ref[...], logits, 0.0), axis=0, keepdims=True)
    out_ref[...] = jnp.concatenate(
        [row_top, row_total, moment, chosen, jnp.zeros((4, row_top.shape[1]), jnp.float32)], axis=0
    )


def slice_stats(rows, ids, head_weight, vocab_ids):
    count, width = rows.shape
    tile = TILE if count % TILE == 0 else count
    slice_width = head_weight.shape[0]
    head = jnp.concatenate(
        [head_weight, jnp.zeros((VOCAB_PAD - slice_width, width), head_weight.dtype)], axis=0
    )
    vocab = jnp.concatenate(
        [vocab_ids, jnp.full((VOCAB_PAD - slice_width,), -1, jnp.int32)]
    )[:, None]
    out = pl.pallas_call(
        stats_kernel,
        grid=(count // tile,),
        in_specs=[
            pl.BlockSpec((VOCAB_PAD, width), lambda i: (0, 0)),
            pl.BlockSpec((VOCAB_PAD, 1), lambda i: (0, 0)),
            pl.BlockSpec((1, tile), lambda i: (0, i)),
            pl.BlockSpec((tile, width), lambda i: (i, 0)),
        ],
        out_specs=pl.BlockSpec((8, tile), lambda i: (0, i)),
        out_shape=jax.ShapeDtypeStruct((8, count), jnp.float32),
        cost_estimate=pl.CostEstimate(
            flops=2 * VOCAB_PAD * width * count,
            transcendentals=VOCAB_PAD * count,
            bytes_accessed=count * width * 2 + VOCAB_PAD * width * 2 + count * 36,
        ),
    )(head, vocab, ids[None, :], rows)
    return out[0], out[1], out[2], out[3]


def norm_kernel(hidden_ref, gain_ref, normed_ref, square_ref):
    widened = hidden_ref[...].astype(jnp.float32)
    mean_square = jnp.mean(widened * widened, axis=1, keepdims=True)
    normed_ref[...] = (
        widened * lax.rsqrt(mean_square + EPSILON) * gain_ref[...].astype(jnp.float32)
    ).astype(normed_ref.dtype)
    square_ref[...] = jnp.broadcast_to(mean_square, square_ref.shape)


def rms_norm(hidden, norm_gain):
    rows, width = hidden.shape
    normed, square = pl.pallas_call(
        norm_kernel,
        out_shape=(
            jax.ShapeDtypeStruct((rows, width), jnp.bfloat16),
            jax.ShapeDtypeStruct((rows, 128), jnp.float32),
        ),
    )(hidden, norm_gain[None, :])
    return normed, square[:, 0]


def shards(hidden, norm_gain, head_weight, targets, lengths, padding_mask, owner_map):
    tok_count = lax.axis_size("tok")
    rep_count = lax.axis_size("rep")
    tok_place = lax.axis_index("tok")
    rep_place = lax.axis_index("rep")
    local_rows, width = hidden.shape
    slice_width = head_weight.shape[0]
    seq_count = lengths.shape[0]

    normed, mean_square = rms_norm(hidden, norm_gain)
    state_norm = jnp.sqrt(mean_square)
    live_row = padding_mask == 1

    gathered = lax.all_gather(normed, "tok", axis=0, tiled=True)
    meta = lax.all_gather(jnp.stack([targets, padding_mask]), "tok", axis=0)
    piece_ids = meta[:, 0, :]
    piece_live = meta[:, 1, :] == 1
    vocab_ids = tok_place * slice_width + jnp.arange(slice_width, dtype=jnp.int32)
    flat_stats = slice_stats(gathered, piece_ids.reshape(-1), head_weight, vocab_ids)
    top_p, total_p, moment_p, chosen_p = (part.reshape(tok_count, local_rows) for part in flat_stats)

    seq_ends = jnp.cumsum(lengths)
    seq_ids = jnp.arange(seq_count, dtype=jnp.int32)
    block_of = jnp.arange(tok_count, dtype=jnp.int32) * rep_count + rep_place
    piece_rows = block_of[:, None] * local_rows + jnp.arange(local_rows, dtype=jnp.int32)[None, :]
    piece_seq = jnp.sum((seq_ends[None, None, :] <= piece_rows[:, :, None]).astype(jnp.int32), axis=2)
    member = (piece_seq[:, :, None] == seq_ids[None, None, :]) & piece_live[:, :, None]
    part_max = jnp.max(jnp.where(member, top_p[:, :, None], NEG_FILL), axis=(0, 1))
    device_place = tok_place * rep_count + rep_place
    own_rows = device_place * local_rows + jnp.arange(local_rows, dtype=jnp.int32)
    part_norm = jnp.sum(
        jnp.where(own_rows[:, None] == seq_ends[None, :] - 1, state_norm[:, None], 0.0), axis=0
    )

    earlier_same = (owner_map[None, :] == owner_map[:, None]) & (seq_ids[None, :] < seq_ids[:, None])
    slot_rank = jnp.sum(earlier_same.astype(jnp.int32), axis=1)
    device_ids = jnp.arange(tok_count * rep_count, dtype=jnp.int32)
    slot_hot = (owner_map[:, None, None] == device_ids[None, :, None]) & (
        slot_rank[:, None, None] == jnp.arange(SLOTS, dtype=jnp.int32)[None, None, :]
    )
    req_max = jnp.max(jnp.where(slot_hot, part_max[:, None, None], NEG_FILL), axis=0)
    req_norm = jnp.sum(jnp.where(slot_hot, part_norm[:, None, None], 0.0), axis=0)
    req = jnp.stack([req_max, req_norm], axis=2).reshape(tok_count, rep_count * SLOTS * 2)

    stats = jnp.stack([top_p, total_p, moment_p, chosen_p], axis=1).reshape(tok_count, local_rows * 4)
    outgoing = jnp.concatenate([stats, req], axis=1)
    incoming = lax.all_to_all(outgoing, "tok", 0, 0, tiled=True)

    in_stats = incoming[:, : local_rows * 4].reshape(tok_count, 4, local_rows)
    tops = in_stats[:, 0, :]
    row_top = jnp.max(tops, axis=0)
    scale = jnp.exp(tops - row_top[None, :])
    row_total = jnp.sum(in_stats[:, 1, :] * scale, axis=0)
    row_moment = jnp.sum(in_stats[:, 2, :] * scale, axis=0)
    row_chosen = jnp.sum(in_stats[:, 3, :], axis=0)
    log_total = jnp.log(row_total)
    logprob = jnp.where(live_row, row_chosen - row_top - log_total, 0.0)
    entropy = jnp.where(live_row, row_top + log_total - row_moment / row_total, 0.0)

    in_req = incoming[:, local_rows * 4:].reshape(tok_count, rep_count, SLOTS, 2)
    rep_max = jnp.max(in_req[..., 0], axis=0)
    rep_norm = jnp.sum(in_req[..., 1], axis=0)
    rep_pair = jnp.stack([rep_max, rep_norm], axis=2)
    got = lax.all_to_all(rep_pair, "rep", 0, 0, tiled=True)
    final_max = jnp.max(got[..., 0], axis=0)
    final_norm = jnp.sum(got[..., 1], axis=0)
    has_slot = jnp.any(slot_hot[:, device_place, :], axis=0)
    request_table = jnp.where(
        has_slot[:, None], jnp.stack([final_max, final_norm], axis=1), 0.0
    )
    return (logprob, entropy, request_table[None])


def solution(mesh):
    return jax.shard_map(
        shards,
        mesh=mesh,
        in_specs=(
            P(("tok", "rep"), None),
            P(),
            P("tok", None),
            P(("tok", "rep")),
            P(),
            P(("tok", "rep")),
            P(),
        ),
        out_specs=(P(("tok", "rep")), P(("tok", "rep")), P(("tok", "rep"), None, None)),
        check_vma=False,
    )
```

```python
import jax
import jax.numpy as jnp
from jax import lax
from jax.experimental import pallas as pl
from jax.experimental.pallas import tpu as pltpu
from jax.experimental.layout import Layout, with_layout_constraint
from jax.sharding import PartitionSpec as P

SLOTS = 2


EPSILON = 1e-06
NEG_FILL = -1e30


TILE = 1536
VOCAB_PAD = 256


def stats_kernel(head_ref, vocab_ref, ids_ref, rows_ref, out_ref):
    logits = lax.dot_general(
        head_ref[...], rows_ref[...], (((1,), (1,)), ((), ())), preferred_element_type=jnp.float32
    )
    logits = jnp.where(vocab_ref[...] >= 0, logits, NEG_FILL)
    row_top = jnp.max(logits, axis=0, keepdims=True)
    weights = jnp.exp(logits - row_top)
    row_total = jnp.sum(weights, axis=0, keepdims=True)
    moment = jnp.sum(weights * logits, axis=0, keepdims=True)
    chosen = jnp.sum(jnp.where(vocab_ref[...] == ids_ref[...], logits, 0.0), axis=0, keepdims=True)
    out_ref[...] = jnp.concatenate(
        [row_top, row_total, moment, chosen, jnp.zeros((4, row_top.shape[1]), jnp.float32)], axis=0
    )


def slice_stats(rows, ids, head_weight, vocab_ids):
    count, width = rows.shape
    tile = TILE if count % TILE == 0 else count
    slice_width = head_weight.shape[0]
    head = jnp.concatenate(
        [head_weight, jnp.zeros((VOCAB_PAD - slice_width, width), head_weight.dtype)], axis=0
    )
    vocab = jnp.concatenate(
        [vocab_ids, jnp.full((VOCAB_PAD - slice_width,), -1, jnp.int32)]
    )[:, None]
    out = pl.pallas_call(
        stats_kernel,
        grid=(count // tile,),
        in_specs=[
            pl.BlockSpec((VOCAB_PAD, width), lambda i: (0, 0)),
            pl.BlockSpec((VOCAB_PAD, 1), lambda i: (0, 0)),
            pl.BlockSpec((1, tile), lambda i: (0, i)),
            pl.BlockSpec((tile, width), lambda i: (i, 0)),
        ],
        out_specs=pl.BlockSpec((8, tile), lambda i: (0, i)),
        out_shape=jax.ShapeDtypeStruct((8, count), jnp.float32),
        cost_estimate=pl.CostEstimate(
            flops=2 * VOCAB_PAD * width * count,
            transcendentals=VOCAB_PAD * count,
            bytes_accessed=count * width * 2 + VOCAB_PAD * width * 2 + count * 36,
        ),
    )(head, vocab, ids[None, :], rows)
    return out[0], out[1], out[2], out[3]


def norm_kernel(hidden_ref, gain_ref, normed_ref, square_ref):
    widened = hidden_ref[...].astype(jnp.float32)
    mean_square = jnp.mean(widened * widened, axis=1, keepdims=True)
    normed_ref[...] = (
        widened * lax.rsqrt(mean_square + EPSILON) * gain_ref[...].astype(jnp.float32)
    ).astype(normed_ref.dtype)
    square_ref[...] = jnp.broadcast_to(mean_square, square_ref.shape)


def rms_norm(hidden, norm_gain):
    rows, width = hidden.shape
    normed, square = pl.pallas_call(
        norm_kernel,
        out_shape=(
            jax.ShapeDtypeStruct((rows, width), jnp.bfloat16),
            jax.ShapeDtypeStruct((rows, 128), jnp.float32),
        ),
    )(hidden, norm_gain[None, :])
    return normed, square[:, 0]


def shards(hidden, norm_gain, head_weight, targets, lengths, padding_mask, owner_map):
    tok_count = lax.axis_size("tok")
    rep_count = lax.axis_size("rep")
    tok_place = lax.axis_index("tok")
    rep_place = lax.axis_index("rep")
    local_rows, width = hidden.shape
    slice_width = head_weight.shape[0]
    seq_count = lengths.shape[0]

    normed, mean_square = rms_norm(hidden, norm_gain)
    state_norm = jnp.sqrt(mean_square)
    live_row = padding_mask == 1

    gathered = lax.all_gather(normed, "tok", axis=0, tiled=True)
    meta = lax.all_gather(jnp.stack([targets, padding_mask]), "tok", axis=0)
    piece_ids = meta[:, 0, :]
    piece_live = meta[:, 1, :] == 1
    vocab_ids = tok_place * slice_width + jnp.arange(slice_width, dtype=jnp.int32)
    flat_stats = slice_stats(gathered, piece_ids.reshape(-1), head_weight, vocab_ids)
    top_p, total_p, moment_p, chosen_p = (part.reshape(tok_count, local_rows) for part in flat_stats)

    seq_ends = jnp.cumsum(lengths)
    seq_ids = jnp.arange(seq_count, dtype=jnp.int32)
    block_of = jnp.arange(tok_count, dtype=jnp.int32) * rep_count + rep_place
    piece_rows = block_of[:, None] * local_rows + jnp.arange(local_rows, dtype=jnp.int32)[None, :]
    piece_seq = jnp.sum((seq_ends[None, None, :] <= piece_rows[:, :, None]).astype(jnp.int32), axis=2)
    member = (piece_seq[:, :, None] == seq_ids[None, None, :]) & piece_live[:, :, None]
    part_max = jnp.max(jnp.where(member, top_p[:, :, None], NEG_FILL), axis=(0, 1))
    device_place = tok_place * rep_count + rep_place
    own_rows = device_place * local_rows + jnp.arange(local_rows, dtype=jnp.int32)
    part_norm = jnp.sum(
        jnp.where(own_rows[:, None] == seq_ends[None, :] - 1, state_norm[:, None], 0.0), axis=0
    )

    earlier_same = (owner_map[None, :] == owner_map[:, None]) & (seq_ids[None, :] < seq_ids[:, None])
    slot_rank = jnp.sum(earlier_same.astype(jnp.int32), axis=1)
    device_ids = jnp.arange(tok_count * rep_count, dtype=jnp.int32)
    slot_hot = (owner_map[:, None, None] == device_ids[None, :, None]) & (
        slot_rank[:, None, None] == jnp.arange(SLOTS, dtype=jnp.int32)[None, None, :]
    )
    req_max = jnp.max(jnp.where(slot_hot, part_max[:, None, None], NEG_FILL), axis=0)
    req_norm = jnp.sum(jnp.where(slot_hot, part_norm[:, None, None], 0.0), axis=0)
    req = jnp.stack([req_max, req_norm], axis=2).reshape(tok_count, rep_count * SLOTS * 2)

    stats = jnp.stack([top_p, total_p, moment_p, chosen_p], axis=2).reshape(tok_count, local_rows * 4)
    outgoing = with_layout_constraint(jnp.concatenate([stats, req], axis=1), Layout((0, 1)))
    incoming = lax.all_to_all(outgoing, "tok", 0, 0, tiled=True)

    in_stats = incoming[:, : local_rows * 4].reshape(tok_count, local_rows, 4)
    tops = in_stats[:, :, 0]
    row_top = jnp.max(tops, axis=0)
    scale = jnp.exp(tops - row_top[None, :])
    row_total = jnp.sum(in_stats[:, :, 1] * scale, axis=0)
    row_moment = jnp.sum(in_stats[:, :, 2] * scale, axis=0)
    row_chosen = jnp.sum(in_stats[:, :, 3], axis=0)
    log_total = jnp.log(row_total)
    logprob = jnp.where(live_row, row_chosen - row_top - log_total, 0.0)
    entropy = jnp.where(live_row, row_top + log_total - row_moment / row_total, 0.0)

    in_req = incoming[:, local_rows * 4:].reshape(tok_count, rep_count, SLOTS, 2)
    rep_max = jnp.max(in_req[..., 0], axis=0)
    rep_norm = jnp.sum(in_req[..., 1], axis=0)
    rep_pair = jnp.stack([rep_max, rep_norm], axis=2)
    got = lax.all_to_all(rep_pair, "rep", 0, 0, tiled=True)
    final_max = jnp.max(got[..., 0], axis=0)
    final_norm = jnp.sum(got[..., 1], axis=0)
    has_slot = jnp.any(slot_hot[:, device_place, :], axis=0)
    request_table = jnp.where(
        has_slot[:, None], jnp.stack([final_max, final_norm], axis=1), 0.0
    )
    return (logprob, entropy, request_table[None])


def solution(mesh):
    return jax.shard_map(
        shards,
        mesh=mesh,
        in_specs=(
            P(("tok", "rep"), None),
            P(),
            P("tok", None),
            P(("tok", "rep")),
            P(),
            P(("tok", "rep")),
            P(),
        ),
        out_specs=(P(("tok", "rep")), P(("tok", "rep")), P(("tok", "rep"), None, None)),
        check_vma=False,
    )
```

```python
import jax
import jax.numpy as jnp
from jax import lax
from jax.experimental import pallas as pl
from jax.experimental.pallas import tpu as pltpu
from jax.experimental.layout import Layout, with_layout_constraint
from jax.sharding import PartitionSpec as P

SLOTS = 2


EPSILON = 1e-06
NEG_FILL = -1e30


TILE = 1536
VOCAB_PAD = 256


def stats_kernel(head_ref, vocab_ref, ids_ref, rows_ref, out_ref):
    logits = lax.dot_general(
        head_ref[...], rows_ref[...], (((1,), (1,)), ((), ())), preferred_element_type=jnp.float32
    )
    logits = jnp.where(vocab_ref[...] >= 0, logits, NEG_FILL)
    row_top = jnp.max(logits, axis=0, keepdims=True)
    weights = jnp.exp(logits - row_top)
    row_total = jnp.sum(weights, axis=0, keepdims=True)
    moment = jnp.sum(weights * logits, axis=0, keepdims=True)
    chosen = jnp.sum(jnp.where(vocab_ref[...] == ids_ref[...], logits, 0.0), axis=0, keepdims=True)
    out_ref[...] = jnp.concatenate(
        [row_top, row_total, moment, chosen, jnp.zeros((4, row_top.shape[1]), jnp.float32)], axis=0
    )


def slice_stats(rows, ids, head_weight, vocab_ids):
    count, width = rows.shape
    tile = TILE if count % TILE == 0 else count
    slice_width = head_weight.shape[0]
    head = jnp.concatenate(
        [head_weight, jnp.zeros((VOCAB_PAD - slice_width, width), head_weight.dtype)], axis=0
    )
    vocab = jnp.concatenate(
        [vocab_ids, jnp.full((VOCAB_PAD - slice_width,), -1, jnp.int32)]
    )[:, None]
    out = pl.pallas_call(
        stats_kernel,
        grid=(count // tile,),
        in_specs=[
            pl.BlockSpec((VOCAB_PAD, width), lambda i: (0, 0)),
            pl.BlockSpec((VOCAB_PAD, 1), lambda i: (0, 0)),
            pl.BlockSpec((1, tile), lambda i: (0, i)),
            pl.BlockSpec((tile, width), lambda i: (i, 0)),
        ],
        out_specs=pl.BlockSpec((8, tile), lambda i: (0, i)),
        out_shape=jax.ShapeDtypeStruct((8, count), jnp.float32),
        cost_estimate=pl.CostEstimate(
            flops=2 * VOCAB_PAD * width * count,
            transcendentals=VOCAB_PAD * count,
            bytes_accessed=count * width * 2 + VOCAB_PAD * width * 2 + count * 36,
        ),
    )(head, vocab, ids[None, :], rows)
    return out[0], out[1], out[2], out[3]


def norm_kernel(hidden_ref, gain_ref, normed_ref, square_ref):
    widened = hidden_ref[...].astype(jnp.float32)
    mean_square = jnp.mean(widened * widened, axis=1, keepdims=True)
    normed_ref[...] = (
        widened * lax.rsqrt(mean_square + EPSILON) * gain_ref[...].astype(jnp.float32)
    ).astype(normed_ref.dtype)
    square_ref[...] = jnp.broadcast_to(mean_square, square_ref.shape)


def rms_norm(hidden, norm_gain):
    rows, width = hidden.shape
    normed, square = pl.pallas_call(
        norm_kernel,
        out_shape=(
            jax.ShapeDtypeStruct((rows, width), jnp.bfloat16),
            jax.ShapeDtypeStruct((rows, 128), jnp.float32),
        ),
    )(hidden, norm_gain[None, :])
    return normed, square[:, 0]


def shards(hidden, norm_gain, head_weight, targets, lengths, padding_mask, owner_map):
    tok_count = lax.axis_size("tok")
    rep_count = lax.axis_size("rep")
    tok_place = lax.axis_index("tok")
    rep_place = lax.axis_index("rep")
    local_rows, width = hidden.shape
    slice_width = head_weight.shape[0]
    seq_count = lengths.shape[0]

    normed, mean_square = rms_norm(hidden, norm_gain)
    state_norm = jnp.sqrt(mean_square)
    live_row = padding_mask == 1

    gathered = lax.all_gather(normed, "tok", axis=0, tiled=True)
    meta = lax.all_gather(jnp.stack([targets, padding_mask]), "tok", axis=0)
    piece_ids = meta[:, 0, :]
    piece_live = meta[:, 1, :] == 1
    vocab_ids = tok_place * slice_width + jnp.arange(slice_width, dtype=jnp.int32)
    flat_stats = slice_stats(gathered, piece_ids.reshape(-1), head_weight, vocab_ids)
    top_p, total_p, moment_p, chosen_p = (part.reshape(tok_count, local_rows) for part in flat_stats)

    seq_ends = jnp.cumsum(lengths)
    seq_ids = jnp.arange(seq_count, dtype=jnp.int32)
    block_of = jnp.arange(tok_count, dtype=jnp.int32) * rep_count + rep_place
    piece_rows = block_of[:, None] * local_rows + jnp.arange(local_rows, dtype=jnp.int32)[None, :]
    piece_seq = jnp.sum((seq_ends[None, None, :] <= piece_rows[:, :, None]).astype(jnp.int32), axis=2)
    member = (piece_seq[:, :, None] == seq_ids[None, None, :]) & piece_live[:, :, None]
    part_max = jnp.max(jnp.where(member, top_p[:, :, None], NEG_FILL), axis=(0, 1))
    device_place = tok_place * rep_count + rep_place
    own_rows = device_place * local_rows + jnp.arange(local_rows, dtype=jnp.int32)
    part_norm = jnp.sum(
        jnp.where(own_rows[:, None] == seq_ends[None, :] - 1, state_norm[:, None], 0.0), axis=0
    )

    earlier_same = (owner_map[None, :] == owner_map[:, None]) & (seq_ids[None, :] < seq_ids[:, None])
    slot_rank = jnp.sum(earlier_same.astype(jnp.int32), axis=1)
    device_ids = jnp.arange(tok_count * rep_count, dtype=jnp.int32)
    slot_hot = (owner_map[:, None, None] == device_ids[None, :, None]) & (
        slot_rank[:, None, None] == jnp.arange(SLOTS, dtype=jnp.int32)[None, None, :]
    )
    req_max = jnp.max(jnp.where(slot_hot, part_max[:, None, None], NEG_FILL), axis=0)
    req_norm = jnp.sum(jnp.where(slot_hot, part_norm[:, None, None], 0.0), axis=0)
    req = jnp.stack([req_max, req_norm], axis=2).reshape(tok_count, rep_count * SLOTS * 2)

    stats = jnp.stack([top_p, total_p, moment_p, chosen_p], axis=2).reshape(tok_count, local_rows * 4)
    outgoing = with_layout_constraint(jnp.concatenate([stats, req], axis=1), Layout((0, 1)))
    incoming = lax.all_to_all(outgoing, "tok", 0, 0, tiled=True)

    in_stats = incoming[:, : local_rows * 4].reshape(tok_count, local_rows, 4)
    tops = in_stats[:, :, 0]
    row_top = jnp.max(tops, axis=0)
    scale = jnp.exp(tops - row_top[None, :])
    row_total = jnp.sum(in_stats[:, :, 1] * scale, axis=0)
    row_moment = jnp.sum(in_stats[:, :, 2] * scale, axis=0)
    row_chosen = jnp.sum(in_stats[:, :, 3], axis=0)
    log_total = jnp.log(row_total)
    logprob = jnp.where(live_row, row_chosen - row_top - log_total, 0.0)
    entropy = jnp.where(live_row, row_top + log_total - row_moment / row_total, 0.0)

    in_req = incoming[:, local_rows * 4:].reshape(tok_count, rep_count, SLOTS, 2)
    rep_max = jnp.max(in_req[..., 0], axis=0)
    rep_norm = jnp.sum(in_req[..., 1], axis=0)
    rep_pair = with_layout_constraint(jnp.stack([rep_max, rep_norm], axis=2), Layout((0, 1, 2)))
    got = lax.all_to_all(rep_pair, "rep", 0, 0, tiled=True)
    final_max = jnp.max(got[..., 0], axis=0)
    final_norm = jnp.sum(got[..., 1], axis=0)
    has_slot = jnp.any(slot_hot[:, device_place, :], axis=0)
    request_table = jnp.where(
        has_slot[:, None], jnp.stack([final_max, final_norm], axis=1), 0.0
    )
    return (logprob, entropy, request_table[None])


def solution(mesh):
    return jax.shard_map(
        shards,
        mesh=mesh,
        in_specs=(
            P(("tok", "rep"), None),
            P(),
            P("tok", None),
            P(("tok", "rep")),
            P(),
            P(("tok", "rep")),
            P(),
        ),
        out_specs=(P(("tok", "rep")), P(("tok", "rep")), P(("tok", "rep"), None, None)),
        check_vma=False,
    )
```

```python
import jax
import jax.numpy as jnp
from jax import lax
from jax.experimental import pallas as pl
from jax.experimental.pallas import tpu as pltpu
from jax.experimental.layout import Layout, with_layout_constraint
from jax.sharding import PartitionSpec as P

SLOTS = 2


EPSILON = 1e-06
NEG_FILL = -1e30


TILE = 3072
VOCAB_PAD = 256


def stats_kernel(head_ref, vocab_ref, ids_ref, rows_ref, out_ref):
    logits = lax.dot_general(
        head_ref[...], rows_ref[...], (((1,), (1,)), ((), ())), preferred_element_type=jnp.float32
    )
    logits = jnp.where(vocab_ref[...] >= 0, logits, NEG_FILL)
    row_top = jnp.max(logits, axis=0, keepdims=True)
    weights = jnp.exp(logits - row_top)
    row_total = jnp.sum(weights, axis=0, keepdims=True)
    moment = jnp.sum(weights * logits, axis=0, keepdims=True)
    chosen = jnp.sum(jnp.where(vocab_ref[...] == ids_ref[...], logits, 0.0), axis=0, keepdims=True)
    out_ref[...] = jnp.concatenate(
        [row_top, row_total, moment, chosen, jnp.zeros((4, row_top.shape[1]), jnp.float32)], axis=0
    )


def slice_stats(rows, ids, head_weight, vocab_ids):
    count, width = rows.shape
    tile = TILE if count % TILE == 0 else count
    slice_width = head_weight.shape[0]
    head = jnp.concatenate(
        [head_weight, jnp.zeros((VOCAB_PAD - slice_width, width), head_weight.dtype)], axis=0
    )
    vocab = jnp.concatenate(
        [vocab_ids, jnp.full((VOCAB_PAD - slice_width,), -1, jnp.int32)]
    )[:, None]
    out = pl.pallas_call(
        stats_kernel,
        grid=(count // tile,),
        in_specs=[
            pl.BlockSpec((VOCAB_PAD, width), lambda i: (0, 0)),
            pl.BlockSpec((VOCAB_PAD, 1), lambda i: (0, 0)),
            pl.BlockSpec((1, tile), lambda i: (0, i)),
            pl.BlockSpec((tile, width), lambda i: (i, 0)),
        ],
        out_specs=pl.BlockSpec((8, tile), lambda i: (0, i)),
        out_shape=jax.ShapeDtypeStruct((8, count), jnp.float32),
        cost_estimate=pl.CostEstimate(
            flops=2 * VOCAB_PAD * width * count,
            transcendentals=VOCAB_PAD * count,
            bytes_accessed=count * width * 2 + VOCAB_PAD * width * 2 + count * 36,
        ),
    )(head, vocab, ids[None, :], rows)
    return out[0], out[1], out[2], out[3]


def norm_kernel(hidden_ref, gain_ref, normed_ref, square_ref):
    widened = hidden_ref[...].astype(jnp.float32)
    mean_square = jnp.mean(widened * widened, axis=1, keepdims=True)
    normed_ref[...] = (
        widened * lax.rsqrt(mean_square + EPSILON) * gain_ref[...].astype(jnp.float32)
    ).astype(normed_ref.dtype)
    square_ref[...] = jnp.broadcast_to(mean_square, square_ref.shape)


def rms_norm(hidden, norm_gain):
    rows, width = hidden.shape
    normed, square = pl.pallas_call(
        norm_kernel,
        out_shape=(
            jax.ShapeDtypeStruct((rows, width), jnp.bfloat16),
            jax.ShapeDtypeStruct((rows, 128), jnp.float32),
        ),
    )(hidden, norm_gain[None, :])
    return normed, square[:, 0]


def shards(hidden, norm_gain, head_weight, targets, lengths, padding_mask, owner_map):
    tok_count = lax.axis_size("tok")
    rep_count = lax.axis_size("rep")
    tok_place = lax.axis_index("tok")
    rep_place = lax.axis_index("rep")
    local_rows, width = hidden.shape
    slice_width = head_weight.shape[0]
    seq_count = lengths.shape[0]

    normed, mean_square = rms_norm(hidden, norm_gain)
    state_norm = jnp.sqrt(mean_square)
    live_row = padding_mask == 1

    gathered = lax.all_gather(normed, "tok", axis=0, tiled=True)
    meta = lax.all_gather(jnp.stack([targets, padding_mask]), "tok", axis=0)
    piece_ids = meta[:, 0, :]
    piece_live = meta[:, 1, :] == 1
    vocab_ids = tok_place * slice_width + jnp.arange(slice_width, dtype=jnp.int32)
    flat_stats = slice_stats(gathered, piece_ids.reshape(-1), head_weight, vocab_ids)
    top_p, total_p, moment_p, chosen_p = (part.reshape(tok_count, local_rows) for part in flat_stats)

    seq_ends = jnp.cumsum(lengths)
    seq_ids = jnp.arange(seq_count, dtype=jnp.int32)
    block_of = jnp.arange(tok_count, dtype=jnp.int32) * rep_count + rep_place
    piece_rows = block_of[:, None] * local_rows + jnp.arange(local_rows, dtype=jnp.int32)[None, :]
    piece_seq = jnp.sum((seq_ends[None, None, :] <= piece_rows[:, :, None]).astype(jnp.int32), axis=2)
    member = (piece_seq[:, :, None] == seq_ids[None, None, :]) & piece_live[:, :, None]
    part_max = jnp.max(jnp.where(member, top_p[:, :, None], NEG_FILL), axis=(0, 1))
    device_place = tok_place * rep_count + rep_place
    own_rows = device_place * local_rows + jnp.arange(local_rows, dtype=jnp.int32)
    part_norm = jnp.sum(
        jnp.where(own_rows[:, None] == seq_ends[None, :] - 1, state_norm[:, None], 0.0), axis=0
    )

    earlier_same = (owner_map[None, :] == owner_map[:, None]) & (seq_ids[None, :] < seq_ids[:, None])
    slot_rank = jnp.sum(earlier_same.astype(jnp.int32), axis=1)
    device_ids = jnp.arange(tok_count * rep_count, dtype=jnp.int32)
    slot_hot = (owner_map[:, None, None] == device_ids[None, :, None]) & (
        slot_rank[:, None, None] == jnp.arange(SLOTS, dtype=jnp.int32)[None, None, :]
    )
    req_max = jnp.max(jnp.where(slot_hot, part_max[:, None, None], NEG_FILL), axis=0)
    req_norm = jnp.sum(jnp.where(slot_hot, part_norm[:, None, None], 0.0), axis=0)
    req = jnp.stack([req_max, req_norm], axis=2).reshape(tok_count, rep_count * SLOTS * 2)

    stats = jnp.stack([top_p, total_p, moment_p, chosen_p], axis=2).reshape(tok_count, local_rows * 4)
    outgoing = with_layout_constraint(jnp.concatenate([stats, req], axis=1), Layout((0, 1)))
    incoming = lax.all_to_all(outgoing, "tok", 0, 0, tiled=True)

    in_stats = incoming[:, : local_rows * 4].reshape(tok_count, local_rows, 4)
    tops = in_stats[:, :, 0]
    row_top = jnp.max(tops, axis=0)
    scale = jnp.exp(tops - row_top[None, :])
    row_total = jnp.sum(in_stats[:, :, 1] * scale, axis=0)
    row_moment = jnp.sum(in_stats[:, :, 2] * scale, axis=0)
    row_chosen = jnp.sum(in_stats[:, :, 3], axis=0)
    log_total = jnp.log(row_total)
    logprob = jnp.where(live_row, row_chosen - row_top - log_total, 0.0)
    entropy = jnp.where(live_row, row_top + log_total - row_moment / row_total, 0.0)

    in_req = incoming[:, local_rows * 4:].reshape(tok_count, rep_count, SLOTS, 2)
    rep_max = jnp.max(in_req[..., 0], axis=0)
    rep_norm = jnp.sum(in_req[..., 1], axis=0)
    rep_pair = jnp.stack([rep_max, rep_norm], axis=2)
    got = lax.all_to_all(rep_pair, "rep", 0, 0, tiled=True)
    final_max = jnp.max(got[..., 0], axis=0)
    final_norm = jnp.sum(got[..., 1], axis=0)
    has_slot = jnp.any(slot_hot[:, device_place, :], axis=0)
    request_table = jnp.where(
        has_slot[:, None], jnp.stack([final_max, final_norm], axis=1), 0.0
    )
    return (logprob, entropy, request_table[None])


def solution(mesh):
    return jax.shard_map(
        shards,
        mesh=mesh,
        in_specs=(
            P(("tok", "rep"), None),
            P(),
            P("tok", None),
            P(("tok", "rep")),
            P(),
            P(("tok", "rep")),
            P(),
        ),
        out_specs=(P(("tok", "rep")), P(("tok", "rep")), P(("tok", "rep"), None, None)),
        check_vma=False,
    )
```

```python
import jax
import jax.numpy as jnp
from jax import lax
from jax.experimental import pallas as pl
from jax.experimental.pallas import tpu as pltpu
from jax.experimental.layout import Layout, with_layout_constraint
from jax.sharding import PartitionSpec as P

SLOTS = 2


EPSILON = 1e-06
NEG_FILL = -1e30


TILE = 1024
VOCAB_PAD = 256


def stats_kernel(head_ref, vocab_ref, ids_ref, rows_ref, out_ref):
    logits = lax.dot_general(
        head_ref[...], rows_ref[...], (((1,), (1,)), ((), ())), preferred_element_type=jnp.float32
    )
    logits = jnp.where(vocab_ref[...] >= 0, logits, NEG_FILL)
    row_top = jnp.max(logits, axis=0, keepdims=True)
    weights = jnp.exp(logits - row_top)
    row_total = jnp.sum(weights, axis=0, keepdims=True)
    moment = jnp.sum(weights * logits, axis=0, keepdims=True)
    chosen = jnp.sum(jnp.where(vocab_ref[...] == ids_ref[...], logits, 0.0), axis=0, keepdims=True)
    out_ref[...] = jnp.concatenate(
        [row_top, row_total, moment, chosen, jnp.zeros((4, row_top.shape[1]), jnp.float32)], axis=0
    )


def slice_stats(rows, ids, head_weight, vocab_ids):
    count, width = rows.shape
    tile = TILE if count % TILE == 0 else count
    slice_width = head_weight.shape[0]
    head = jnp.concatenate(
        [head_weight, jnp.zeros((VOCAB_PAD - slice_width, width), head_weight.dtype)], axis=0
    )
    vocab = jnp.concatenate(
        [vocab_ids, jnp.full((VOCAB_PAD - slice_width,), -1, jnp.int32)]
    )[:, None]
    out = pl.pallas_call(
        stats_kernel,
        grid=(count // tile,),
        in_specs=[
            pl.BlockSpec((VOCAB_PAD, width), lambda i: (0, 0)),
            pl.BlockSpec((VOCAB_PAD, 1), lambda i: (0, 0)),
            pl.BlockSpec((1, tile), lambda i: (0, i)),
            pl.BlockSpec((tile, width), lambda i: (i, 0)),
        ],
        out_specs=pl.BlockSpec((8, tile), lambda i: (0, i)),
        out_shape=jax.ShapeDtypeStruct((8, count), jnp.float32),
        cost_estimate=pl.CostEstimate(
            flops=2 * VOCAB_PAD * width * count,
            transcendentals=VOCAB_PAD * count,
            bytes_accessed=count * width * 2 + VOCAB_PAD * width * 2 + count * 36,
        ),
    )(head, vocab, ids[None, :], rows)
    return out[0], out[1], out[2], out[3]


def norm_kernel(hidden_ref, gain_ref, normed_ref, square_ref):
    widened = hidden_ref[...].astype(jnp.float32)
    mean_square = jnp.mean(widened * widened, axis=1, keepdims=True)
    normed_ref[...] = (
        widened * lax.rsqrt(mean_square + EPSILON) * gain_ref[...].astype(jnp.float32)
    ).astype(normed_ref.dtype)
    square_ref[...] = jnp.broadcast_to(mean_square, square_ref.shape)


def rms_norm(hidden, norm_gain):
    rows, width = hidden.shape
    normed, square = pl.pallas_call(
        norm_kernel,
        out_shape=(
            jax.ShapeDtypeStruct((rows, width), jnp.bfloat16),
            jax.ShapeDtypeStruct((rows, 128), jnp.float32),
        ),
    )(hidden, norm_gain[None, :])
    return normed, square[:, 0]


def shards(hidden, norm_gain, head_weight, targets, lengths, padding_mask, owner_map):
    tok_count = lax.axis_size("tok")
    rep_count = lax.axis_size("rep")
    tok_place = lax.axis_index("tok")
    rep_place = lax.axis_index("rep")
    local_rows, width = hidden.shape
    slice_width = head_weight.shape[0]
    seq_count = lengths.shape[0]

    normed, mean_square = rms_norm(hidden, norm_gain)
    state_norm = jnp.sqrt(mean_square)
    live_row = padding_mask == 1

    gathered = lax.all_gather(normed, "tok", axis=0, tiled=True)
    meta = lax.all_gather(jnp.stack([targets, padding_mask]), "tok", axis=0)
    piece_ids = meta[:, 0, :]
    piece_live = meta[:, 1, :] == 1
    vocab_ids = tok_place * slice_width + jnp.arange(slice_width, dtype=jnp.int32)
    flat_stats = slice_stats(gathered, piece_ids.reshape(-1), head_weight, vocab_ids)
    top_p, total_p, moment_p, chosen_p = (part.reshape(tok_count, local_rows) for part in flat_stats)

    seq_ends = jnp.cumsum(lengths)
    seq_ids = jnp.arange(seq_count, dtype=jnp.int32)
    block_of = jnp.arange(tok_count, dtype=jnp.int32) * rep_count + rep_place
    piece_rows = block_of[:, None] * local_rows + jnp.arange(local_rows, dtype=jnp.int32)[None, :]
    piece_seq = jnp.sum((seq_ends[None, None, :] <= piece_rows[:, :, None]).astype(jnp.int32), axis=2)
    member = (piece_seq[:, :, None] == seq_ids[None, None, :]) & piece_live[:, :, None]
    part_max = jnp.max(jnp.where(member, top_p[:, :, None], NEG_FILL), axis=(0, 1))
    device_place = tok_place * rep_count + rep_place
    own_rows = device_place * local_rows + jnp.arange(local_rows, dtype=jnp.int32)
    part_norm = jnp.sum(
        jnp.where(own_rows[:, None] == seq_ends[None, :] - 1, state_norm[:, None], 0.0), axis=0
    )

    earlier_same = (owner_map[None, :] == owner_map[:, None]) & (seq_ids[None, :] < seq_ids[:, None])
    slot_rank = jnp.sum(earlier_same.astype(jnp.int32), axis=1)
    device_ids = jnp.arange(tok_count * rep_count, dtype=jnp.int32)
    slot_hot = (owner_map[:, None, None] == device_ids[None, :, None]) & (
        slot_rank[:, None, None] == jnp.arange(SLOTS, dtype=jnp.int32)[None, None, :]
    )
    req_max = jnp.max(jnp.where(slot_hot, part_max[:, None, None], NEG_FILL), axis=0)
    req_norm = jnp.sum(jnp.where(slot_hot, part_norm[:, None, None], 0.0), axis=0)
    req = jnp.stack([req_max, req_norm], axis=2).reshape(tok_count, rep_count * SLOTS * 2)

    stats = jnp.stack([top_p, total_p, moment_p, chosen_p], axis=2).reshape(tok_count, local_rows * 4)
    outgoing = with_layout_constraint(jnp.concatenate([stats, req], axis=1), Layout((0, 1)))
    incoming = lax.all_to_all(outgoing, "tok", 0, 0, tiled=True)

    in_stats = incoming[:, : local_rows * 4].reshape(tok_count, local_rows, 4)
    tops = in_stats[:, :, 0]
    row_top = jnp.max(tops, axis=0)
    scale = jnp.exp(tops - row_top[None, :])
    row_total = jnp.sum(in_stats[:, :, 1] * scale, axis=0)
    row_moment = jnp.sum(in_stats[:, :, 2] * scale, axis=0)
    row_chosen = jnp.sum(in_stats[:, :, 3], axis=0)
    log_total = jnp.log(row_total)
    logprob = jnp.where(live_row, row_chosen - row_top - log_total, 0.0)
    entropy = jnp.where(live_row, row_top + log_total - row_moment / row_total, 0.0)

    in_req = incoming[:, local_rows * 4:].reshape(tok_count, rep_count, SLOTS, 2)
    rep_max = jnp.max(in_req[..., 0], axis=0)
    rep_norm = jnp.sum(in_req[..., 1], axis=0)
    rep_pair = jnp.stack([rep_max, rep_norm], axis=2)
    got = lax.all_to_all(rep_pair, "rep", 0, 0, tiled=True)
    final_max = jnp.max(got[..., 0], axis=0)
    final_norm = jnp.sum(got[..., 1], axis=0)
    has_slot = jnp.any(slot_hot[:, device_place, :], axis=0)
    request_table = jnp.where(
        has_slot[:, None], jnp.stack([final_max, final_norm], axis=1), 0.0
    )
    return (logprob, entropy, request_table[None])


def solution(mesh):
    return jax.shard_map(
        shards,
        mesh=mesh,
        in_specs=(
            P(("tok", "rep"), None),
            P(),
            P("tok", None),
            P(("tok", "rep")),
            P(),
            P(("tok", "rep")),
            P(),
        ),
        out_specs=(P(("tok", "rep")), P(("tok", "rep")), P(("tok", "rep"), None, None)),
        check_vma=False,
    )
```
